256 devices in a mesh: seq: 8 (over z_lo, core), blk: 32 (over y, z_hi, x).
Axes of the slice: x: 4, y: 4, z: 8 (z_hi: 2, z_lo: 4; z = z_hi * 4 + z_lo), core: 2. Of those that a mesh axis runs over, the one named last changes fastest.
Arguments:
- stream: float32 [4096, 3072], P(('seq', 'blk')), may hold values from -39 to 39
- key_keep: int32 [4096], replicated, may hold values 0 or 1
- positions: int32 [4096, 3], replicated, may hold values from 0 to 63
- lengths: int32 [4], replicated, may hold values from 1 to 2048, 4096 in all
- step_index: int32 [4], replicated, may hold values from 0 to 27
- mod_table: bfloat16 [4, 28, 3, 3072], replicated, may hold values from -4 to 4
- w_qkv: bfloat16 [3072, 9216], P(None, 'blk'), may hold values from -0.109375 to 0.109375
- w_mlp_in: bfloat16 [3072, 12288], P(None, 'blk'), may hold values from -0.109375 to 0.109375
- q_gain: float32 [128], replicated, may hold values from 0.5 to 10
- k_gain: float32 [128], replicated, may hold values from 0.5 to 10
- w_attn_out: bfloat16 [3072, 3072], P('blk'), may hold values from -0.109375 to 0.109375
- w_mlp_out: bfloat16 [12288, 3072], P('blk'), may hold values from -0.0546875 to 0.0546875
Outputs:
- stream_next: float32 [4096, 3072], P(('seq', 'blk'))
The draws below stay inside these ranges and needn't reach their ends.
Inputs may be any that keep to these rules, and one draw needn't show every extreme that they name: The lengths sum to 4096; the longest request has exactly 2048 tokens.
All inputs are finite; a program needn't handle non-finite values.
Results may differ from the reference program's by a relative error of at most 0.0082.
The reference program's roundings to bfloat16 on the way count: a program that leaves them out, or rounds other values in their place, can miss the bound.
Values may be sent and summed in bfloat16 or wider, within the bound.
No kernel may reach another device: no remote copies, remote signals or barrier semaphores. Data moves between devices by JAX's collectives and lax.ppermute only.
A program may use at most 64 MiB of HBM per device.

```python
import math
import jax
import jax.numpy as jnp
import numpy as np
from jax import lax

D = 3072
HEADS = 24
HD = 128
FF = 12288
REQ = 4
STEPS = 28
TOKENS = 4096
MOST = 2048


def draw_stream(key, part):
    key_base = jax.random.fold_in(key, 10)
    key_norm, key_rows, key_cols = jax.random.split(key_base, 3)
    base_vals = jnp.clip(jax.random.normal(key_norm, (TOKENS, D), jnp.float32), -4.0, 4.0)
    row_scale = jnp.exp(jax.random.uniform(key_rows, (TOKENS, 1), jnp.float32, math.log(0.3), math.log(3.0)))
    col_scale = jnp.exp(jax.random.uniform(key_cols, (1, D), jnp.float32, math.log(0.3), math.log(3.0)))
    result = base_vals * row_scale * col_scale
    return result


def gain_draw(key, salt):
    key_gain = jax.random.fold_in(key, salt)
    low_end, high_end = (0.5, 2.5)
    return jnp.exp(jax.random.uniform(key_gain, (HD,), jnp.float32, math.log(low_end), math.log(high_end)))


def draw_q_gain(key, part):
    return gain_draw(key, 11)


def draw_k_gain(key, part):
    return gain_draw(key, 12)


def place_ends(entries, key, smallest, top_value):
    spot = [jax.random.randint(jax.random.fold_in(key, axis), (), 0, length) for axis, length in enumerate(entries.shape)]
    main_axis = entries.shape.index(max(entries.shape))
    neighbour = spot[:main_axis] + [(spot[main_axis] + 1) % entries.shape[main_axis]] + spot[main_axis + 1:]
    return entries.at[tuple(spot)].set(smallest).at[tuple(neighbour)].set(top_value)


def block_levels(rng, dims, cuts, low, largest):
    level = 1.0
    for axis_at, shards_of in cuts:
        heights = jax.random.uniform(jax.random.fold_in(jax.random.fold_in(rng, 6), axis_at), (shards_of,), jnp.float32, low / len(cuts), largest / len(cuts))
        level = level * jnp.repeat(jnp.exp(heights), dims[axis_at] // shards_of).reshape((-1,) + (1,) * (len(dims) - 1 - axis_at))
    return level


def profile(count, total, bound, lean):
    weights = [(1 << 20) // math.isqrt(standing ** lean) + 1 for standing in range(2, count + 1)]
    rest, given = total - bound - (count - 1), [1] * (count - 1)
    while rest > 0:
        free = [i for i in range(count - 1) if given[i] < bound]
        whole, left = sum([weights[i] for i in free]), rest
        for i in free:
            addition = min(bound - given[i], max(1, left * weights[i] // whole), rest)
            given[i] = given[i] + addition
            rest = rest - addition
    return np.array([bound] + given)


def uneven_parts(stream_key, amount, total, most, skew):
    if amount == 2:
        one = jax.random.randint(stream_key, (), max(1, total - most), min(most, total - 1) + 1)
        return jnp.stack([one, total - one])
    sizes = jnp.asarray(profile(amount, total, most, skew), jnp.int32)
    twos = (amount - 1) // 2
    giver, receiver = sizes[1:1 + 2 * twos:2], sizes[2:2 + 2 * twos:2]
    room = jnp.minimum(giver - 1, most - receiver)
    shifted = jax.random.randint(jax.random.fold_in(stream_key, 1), (twos,), 0, 1 << 20) % (room + 1)
    sizes = sizes.at[1:1 + 2 * twos:2].set(giver - shifted).at[2:2 + 2 * twos:2].set(receiver + shifted)
    return sizes[jax.random.permutation(jax.random.fold_in(stream_key, 2), amount)]


def normal_values(key, extent, spread, bound, cuts=(), kind=jnp.bfloat16):
    gain = block_levels(key, extent, cuts, -0.22, 0.18) if cuts else 1.0
    values = jax.random.normal(key, extent, jnp.float32) * spread * gain
    return jnp.minimum(jnp.maximum(values, -bound), bound).astype(kind)


def setup_inputs(seed: int = 0) -> dict:
    key_list = jax.random.split(jax.random.key(seed), 13)
    return {
        "stream": draw_stream(jax.random.fold_in(key_list[12], 71), 0),
        "key_keep": place_ends((jax.random.randint(key_list[1], (TOKENS,), 0, 4) < 3).astype(jnp.int32), jax.random.fold_in(key_list[1], 1), 0, 1),
        "positions": place_ends(jax.random.randint(key_list[2], (TOKENS, 3), 0, 64), jax.random.fold_in(key_list[2], 1), 0, 63).astype(jnp.int32),
        "lengths": uneven_parts(key_list[3], REQ, TOKENS, MOST, 2).astype(jnp.int32),
        "step_index": place_ends(jax.random.randint(key_list[4], (REQ,), 0, STEPS), jax.random.fold_in(key_list[4], 1), 0, STEPS - 1).astype(jnp.int32),
        "mod_table": normal_values(key_list[5], (REQ, STEPS, 3, D), 0.7, 4.0),
        "w_qkv": normal_values(key_list[6], (D, 3 * D), D ** -0.5, 0.109375, ((1, 32),)),
        "w_mlp_in": normal_values(key_list[7], (D, FF), D ** -0.5, 0.109375, ((1, 32),)),
        "q_gain": draw_q_gain(jax.random.fold_in(key_list[12], 71), 0),
        "k_gain": draw_k_gain(jax.random.fold_in(key_list[12], 71), 0),
        "w_attn_out": normal_values(key_list[10], (D, D), D ** -0.5, 0.109375, ((0, 32),)),
        "w_mlp_out": normal_values(key_list[11], (FF, D), FF ** -0.5, 0.0546875, ((0, 32),)),
    }


def rope_table(head_size):
    first_count = head_size // 16
    second = 7 * head_size // 32
    pair_ids = jnp.arange(head_size // 2, dtype=jnp.int32)
    pair_axis = jnp.where(pair_ids < first_count, 0, jnp.where(pair_ids < first_count + second, 1, 2))
    pair_local = jnp.where(pair_ids < first_count, pair_ids, jnp.where(pair_ids < first_count + second, pair_ids - first_count, pair_ids - first_count - second))
    axis_dims = jnp.where(pair_axis == 0, 2 * first_count, 2 * second)
    frequency = jnp.power(jnp.float32(10000.0), -(2 * pair_local).astype(jnp.float32) / axis_dims.astype(jnp.float32))
    return jnp.where(jnp.arange(3)[:, None] == pair_axis[None, :], frequency[None, :], jnp.float32(0.0))

def angles_of(places, freq_table):
    return lax.optimization_barrier(jnp.sum(places.astype(jnp.float32)[:, :, None] * freq_table[None, :, :], axis=1))

def rotate(values, angles):
    paired = values.reshape(values.shape[:-1] + (values.shape[-1] // 2, 2))
    even_part = paired[..., 0]
    odd_part = paired[..., 1]
    cos_part = jnp.cos(angles)[:, None, :]
    sin_part = jnp.sin(angles)[:, None, :]
    turned = jnp.stack([cos_part * even_part - sin_part * odd_part, sin_part * even_part + cos_part * odd_part], axis=-1)
    return turned.reshape(values.shape)

def rms_scale(values, gain_vec):
    return values * lax.rsqrt(lax.optimization_barrier(jnp.mean(values * values, axis=-1, keepdims=True)) + 1e-06) * gain_vec

def reference(stream, key_keep, positions, lengths, step_index, mod_table, w_qkv, w_mlp_in, q_gain, k_gain, w_attn_out, w_mlp_out):
    token_ids = jnp.arange(TOKENS, dtype=jnp.int32)
    request_ends = jnp.cumsum(lengths).astype(jnp.int32)
    request_of = lax.optimization_barrier(jnp.sum((token_ids[:, None] >= request_ends[None, :]).astype(jnp.int32), axis=1))
    step_pick = (jnp.arange(STEPS, dtype=jnp.int32)[None, :] == step_index[:, None]).astype(jnp.float32)
    modulation = jnp.einsum('rs,rsk->rk', step_pick, mod_table.reshape(REQ, STEPS, 3 * D).astype(jnp.float32))
    member = (request_of[:, None] == jnp.arange(REQ, dtype=jnp.int32)[None, :]).astype(jnp.float32)
    token_mod = jnp.dot(member, modulation, precision=lax.Precision.HIGHEST)
    mod_shift = token_mod[:, :D]
    mod_scale = token_mod[:, D:2 * D]
    mod_gate = token_mod[:, 2 * D:]
    row_mean = lax.optimization_barrier(jnp.mean(stream, axis=1, keepdims=True))
    centered = stream - row_mean
    row_var = lax.optimization_barrier(jnp.mean(centered * centered, axis=1, keepdims=True))
    normed = centered * lax.rsqrt(row_var + 1e-06)
    modin = ((1.0 + mod_scale) * normed + mod_shift).astype(jnp.bfloat16)
    qkv = jnp.dot(modin, w_qkv, preferred_element_type=jnp.float32).astype(jnp.bfloat16)
    mlp_act = jax.nn.gelu(jnp.dot(modin, w_mlp_in, preferred_element_type=jnp.float32), approximate=True).astype(jnp.bfloat16)
    heads4 = qkv.reshape(TOKENS, HEADS, 3, HD)
    angles = angles_of(positions, rope_table(HD))
    query_rot = rotate(rms_scale(heads4[:, :, 0].astype(jnp.float32), q_gain), angles).astype(jnp.bfloat16)
    key_rot = rotate(rms_scale(heads4[:, :, 1].astype(jnp.float32), k_gain), angles).astype(jnp.bfloat16)
    value_rows = heads4[:, :, 2]
    kept = key_keep == 1
    visible = (request_of[:, None] == request_of[None, :]) & (kept[None, :] | (token_ids[:, None] == token_ids[None, :]))
    inv_root = 1.0 / math.sqrt(HD)

    def one_head(inputs):
        query_h, key_h, value_h = inputs
        scores = jnp.dot(query_h, key_h.T, preferred_element_type=jnp.float32) * inv_root
        row_high = lax.optimization_barrier(jnp.max(jnp.where(visible, scores, -1e+30), axis=1))
        weights = jnp.where(visible, jnp.exp(scores - row_high[:, None]), 0.0)
        totals = lax.optimization_barrier(jnp.sum(weights, axis=1))
        mixed = jnp.dot(weights.astype(jnp.bfloat16), value_h, preferred_element_type=jnp.float32)
        return (mixed / totals[:, None]).astype(jnp.bfloat16)
    attended = lax.map(one_head, (query_rot.transpose(1, 0, 2), key_rot.transpose(1, 0, 2), value_rows.transpose(1, 0, 2)))
    attended = attended.transpose(1, 0, 2).reshape(TOKENS, D)
    summed = jnp.dot(attended, w_attn_out, preferred_element_type=jnp.float32) + jnp.dot(mlp_act, w_mlp_out, preferred_element_type=jnp.float32)
    return stream + mod_gate * summed
```

```python
import math

import jax
import jax.numpy as jnp
from jax import lax
from jax.sharding import PartitionSpec as P


def rope_table(head_size):
    first_count = head_size // 16
    second = 7 * head_size // 32
    pair_ids = jnp.arange(head_size // 2, dtype=jnp.int32)
    pair_axis = jnp.where(
        pair_ids < first_count, 0, jnp.where(pair_ids < first_count + second, 1, 2)
    )
    pair_local = jnp.where(
        pair_ids < first_count,
        pair_ids,
        jnp.where(
            pair_ids < first_count + second, pair_ids - first_count, pair_ids - first_count - second
        ),
    )
    axis_dims = jnp.where(pair_axis == 0, 2 * first_count, 2 * second)
    frequency = jnp.power(
        jnp.float32(10000.0), -(2 * pair_local).astype(jnp.float32) / axis_dims.astype(jnp.float32)
    )
    return jnp.where(
        jnp.arange(3)[:, None] == pair_axis[None, :], frequency[None, :], jnp.float32(0.0)
    )


def angles_of(places, freq_table):
    return jnp.sum(places.astype(jnp.float32)[:, :, None] * freq_table[None, :, :], axis=1)


def rotate(values, angles):
    paired = values.reshape(values.shape[:-1] + (values.shape[-1] // 2, 2))
    even_part = paired[..., 0]
    odd_part = paired[..., 1]
    cos_part = jnp.cos(angles)[:, None, :]
    sin_part = jnp.sin(angles)[:, None, :]
    turned = jnp.stack(
        [cos_part * even_part - sin_part * odd_part, sin_part * even_part + cos_part * odd_part],
        axis=-1,
    )
    return turned.reshape(values.shape)


def rms_scale(values, gain_vec):
    return values * lax.rsqrt(jnp.mean(values * values, axis=-1, keepdims=True) + 1e-06) * gain_vec


def segment_of(row_ids, request_ends):
    return jnp.sum((row_ids[:, None] >= request_ends[None, :]).astype(jnp.int32), axis=1)


def spread_rows(row_ids, query_rows, block_rows, tok_seq):
    owner = row_ids // query_rows
    within = row_ids % query_rows
    return within // block_rows * tok_seq + owner * block_rows + within % block_rows


def body(
    stream,
    key_keep,
    positions,
    lengths,
    step_index,
    mod_table,
    w_qkv,
    w_mlp_in,
    q_gain,
    k_gain,
    w_attn_out,
    w_mlp_out,
):
    blk_count = lax.axis_size("blk")
    seq_count = lax.axis_size("seq")
    seq_at = lax.axis_index("seq")
    blk_at = lax.axis_index("blk")
    block_rows = stream.shape[0]
    width = stream.shape[1]
    tok_seq = block_rows * blk_count
    head_size = q_gain.shape[0]
    local_heads = width // head_size // seq_count
    requests = mod_table.shape[0]
    step_total = mod_table.shape[1]
    inv_root = 1.0 / math.sqrt(head_size)
    request_ends = jnp.cumsum(lengths)
    own_rows = seq_at * tok_seq + blk_at * block_rows + jnp.arange(block_rows, dtype=jnp.int32)
    own_request = segment_of(own_rows, request_ends)
    step_pick = (jnp.arange(step_total, dtype=jnp.int32)[None, :] == step_index[:, None]).astype(
        jnp.bfloat16
    )
    modulation = jnp.einsum(
        "rs,rsk->rk",
        step_pick,
        mod_table.reshape(requests, step_total, 3 * width),
        preferred_element_type=jnp.float32,
    )
    member = (own_request[:, None] == jnp.arange(requests, dtype=jnp.int32)[None, :]).astype(
        jnp.float32
    )
    token_mod = jnp.dot(member, modulation, precision=lax.Precision.HIGHEST)
    mod_shift = token_mod[:, :width]
    mod_scale = token_mod[:, width : 2 * width]
    mod_gate = token_mod[:, 2 * width :]
    row_mean = jnp.mean(stream, axis=1, keepdims=True)
    centered = stream - row_mean
    row_var = jnp.mean(centered * centered, axis=1, keepdims=True)
    normed = centered * lax.rsqrt(row_var + 1e-06)
    modin = ((1.0 + mod_scale) * normed + mod_shift).astype(jnp.bfloat16)
    qkv_width = w_qkv.shape[1]
    shard_rows = lax.all_to_all(
        jnp.broadcast_to(modin[None], (blk_count,) + modin.shape), "blk", 0, 0, tiled=True
    ).reshape(blk_count * block_rows, width)
    qkv_part = jnp.dot(shard_rows, w_qkv, preferred_element_type=jnp.float32).astype(jnp.bfloat16)
    mlp_part = jax.nn.gelu(
        jnp.dot(shard_rows, w_mlp_in, preferred_element_type=jnp.float32), approximate=True
    ).astype(jnp.bfloat16)
    joined = jnp.concatenate([qkv_part, mlp_part], axis=1)
    qkv_cols = joined[:, :qkv_width]
    mlp_act = joined[:, qkv_width:]
    heads_in = lax.all_to_all(
        lax.all_to_all(qkv_cols, "blk", split_axis=0, concat_axis=1, tiled=True),
        "seq",
        split_axis=1,
        concat_axis=0,
        tiled=True,
    )
    query_rows = heads_in.shape[0]
    heads4 = heads_in.reshape(query_rows, local_heads, 3, head_size)
    query_ids = spread_rows(
        blk_at * query_rows + jnp.arange(query_rows, dtype=jnp.int32),
        query_rows,
        block_rows,
        tok_seq,
    )
    query_request = segment_of(query_ids, request_ends)
    angles = angles_of(jnp.take(positions, query_ids, axis=0), rope_table(head_size))
    query_rot = rotate(rms_scale(heads4[:, :, 0].astype(jnp.float32), q_gain), angles).astype(
        jnp.bfloat16
    )
    key_rot = rotate(rms_scale(heads4[:, :, 1].astype(jnp.float32), k_gain), angles).astype(
        jnp.bfloat16
    )
    value_rows = heads4[:, :, 2]
    run_top = jnp.full((query_rows, local_heads), -1e30, jnp.float32)
    key_part = lax.all_gather(key_rot, "blk", axis=0, tiled=True)
    value_part = lax.all_gather(value_rows, "blk", axis=0, tiled=True)
    key_ids = spread_rows(
        jnp.arange(key_part.shape[0], dtype=jnp.int32), query_rows, block_rows, tok_seq
    )
    key_request = segment_of(key_ids, request_ends)
    kept = jnp.take(key_keep, key_ids) == 1
    visible = (
        (query_request[:, None] == key_request[None, :])
        & (kept[None, :] | (query_ids[:, None] == key_ids[None, :]))
    )[:, None, :]
    scores = (
        jnp.einsum("qhd,khd->qhk", query_rot, key_part, preferred_element_type=jnp.float32)
        * inv_root
    )
    row_high = jnp.max(jnp.where(visible, scores, -1e30), axis=2)
    new_top = jnp.maximum(run_top, row_high)
    weights = jnp.where(visible, jnp.exp(scores - new_top[:, :, None]), 0.0)
    run_norm = jnp.sum(weights, axis=2)
    run_sum = jnp.einsum(
        "qhk,khd->qhd", weights.astype(jnp.bfloat16), value_part, preferred_element_type=jnp.float32
    )
    run_top, run_norm, run_sum = (new_top, run_norm, run_sum)
    attended = (run_sum / run_norm[:, :, None]).astype(jnp.bfloat16)
    attended = attended.reshape(query_rows, local_heads * head_size)
    attn_local = lax.all_to_all(
        lax.all_to_all(attended, "seq", split_axis=0, concat_axis=1, tiled=True),
        "blk",
        split_axis=1,
        concat_axis=0,
        tiled=True,
    )
    mlp_part = mlp_act
    partial = (
        jnp.dot(attn_local, w_attn_out, preferred_element_type=jnp.float32)
        + jnp.dot(mlp_part, w_mlp_out, preferred_element_type=jnp.float32)
    ).astype(jnp.bfloat16)
    pieces = lax.all_to_all(
        partial.reshape(blk_count, block_rows, width), "blk", 0, 0, tiled=True
    )
    summed = jnp.sum(pieces.astype(jnp.float32), axis=0)
    return stream + mod_gate * summed


def solution(mesh):
    in_specs = (
        P(("seq", "blk"), None),
        P(),
        P(),
        P(),
        P(),
        P(),
        P(None, "blk"),
        P(None, "blk"),
        P(),
        P(),
        P("blk", None),
        P("blk", None),
    )
    out_specs = P(("seq", "blk"), None)
    return jax.shard_map(body, mesh=mesh, in_specs=in_specs, out_specs=out_specs, check_vma=False)
```

```python
import math

import jax
import jax.numpy as jnp
from jax import lax
from jax.sharding import PartitionSpec as P


def rope_table(head_size):
    first_count = head_size // 16
    second = 7 * head_size // 32
    pair_ids = jnp.arange(head_size // 2, dtype=jnp.int32)
    pair_axis = jnp.where(
        pair_ids < first_count, 0, jnp.where(pair_ids < first_count + second, 1, 2)
    )
    pair_local = jnp.where(
        pair_ids < first_count,
        pair_ids,
        jnp.where(
            pair_ids < first_count + second, pair_ids - first_count, pair_ids - first_count - second
        ),
    )
    axis_dims = jnp.where(pair_axis == 0, 2 * first_count, 2 * second)
    frequency = jnp.power(
        jnp.float32(10000.0), -(2 * pair_local).astype(jnp.float32) / axis_dims.astype(jnp.float32)
    )
    return jnp.where(
        jnp.arange(3)[:, None] == pair_axis[None, :], frequency[None, :], jnp.float32(0.0)
    )


def angles_of(places, freq_table):
    return jnp.sum(places.astype(jnp.float32)[:, :, None] * freq_table[None, :, :], axis=1)


def rotate(values, angles):
    paired = values.reshape(values.shape[:-1] + (values.shape[-1] // 2, 2))
    even_part = paired[..., 0]
    odd_part = paired[..., 1]
    cos_part = jnp.cos(angles)[:, None, :]
    sin_part = jnp.sin(angles)[:, None, :]
    turned = jnp.stack(
        [cos_part * even_part - sin_part * odd_part, sin_part * even_part + cos_part * odd_part],
        axis=-1,
    )
    return turned.reshape(values.shape)


def rms_scale(values, gain_vec):
    return values * lax.rsqrt(jnp.mean(values * values, axis=-1, keepdims=True) + 1e-06) * gain_vec


def segment_of(row_ids, request_ends):
    return jnp.sum((row_ids[:, None] >= request_ends[None, :]).astype(jnp.int32), axis=1)


def spread_rows(row_ids, query_rows, block_rows, tok_seq):
    owner = row_ids // query_rows
    within = row_ids % query_rows
    return within // block_rows * tok_seq + owner * block_rows + within % block_rows


SEQ = ("zl", "core")
BLK = ("y", "zh", "x")
PLANE = ("y", "x")
SWAP = [(0, 1), (1, 0)]


def by_half(mine, other):
    first = lax.axis_index("zh") == 0
    return jnp.where(first, mine, other), jnp.where(first, other, mine)


def gather_blk(x):
    low, high = by_half(x, lax.ppermute(x, "zh", SWAP))
    pair = jnp.stack([low, high])
    plane = lax.axis_size("y") * lax.axis_size("x")
    got = lax.all_to_all(jnp.broadcast_to(pair[None], (plane,) + pair.shape), PLANE, 0, 0, tiled=True)
    got = got.reshape((lax.axis_size("y"), lax.axis_size("x"), 2) + x.shape)
    return jnp.swapaxes(got, 1, 2).reshape((-1,) + x.shape[1:])


def reduce_blk(y):
    ys, xs = lax.axis_size("y"), lax.axis_size("x")
    rows = y.shape[0] // (ys * 2 * xs)
    pieces = jnp.swapaxes(y.reshape((ys, 2, xs, rows) + y.shape[1:]), 1, 2)
    pieces = pieces.reshape((ys * xs, 2, rows) + y.shape[1:])
    got = lax.all_to_all(pieces, PLANE, 0, 0, tiled=True)
    part = jnp.sum(got.astype(jnp.float32), axis=0)
    mine, theirs = by_half(part[0], part[1])
    return mine + lax.ppermute(theirs, "zh", SWAP)


def body(
    stream,
    key_keep,
    positions,
    lengths,
    step_index,
    mod_table,
    w_qkv,
    w_mlp_in,
    q_gain,
    k_gain,
    w_attn_out,
    w_mlp_out,
):
    blk_count = lax.axis_size(BLK)
    seq_count = lax.axis_size(SEQ)
    seq_at = lax.axis_index(SEQ)
    blk_at = lax.axis_index(BLK)
    block_rows = stream.shape[0]
    width = stream.shape[1]
    tok_seq = block_rows * blk_count
    head_size = q_gain.shape[0]
    local_heads = width // head_size // seq_count
    requests = mod_table.shape[0]
    step_total = mod_table.shape[1]
    inv_root = 1.0 / math.sqrt(head_size)
    request_ends = jnp.cumsum(lengths)
    own_rows = seq_at * tok_seq + blk_at * block_rows + jnp.arange(block_rows, dtype=jnp.int32)
    own_request = segment_of(own_rows, request_ends)
    step_pick = (jnp.arange(step_total, dtype=jnp.int32)[None, :] == step_index[:, None]).astype(
        jnp.bfloat16
    )
    modulation = jnp.einsum(
        "rs,rsk->rk",
        step_pick,
        mod_table.reshape(requests, step_total, 3 * width),
        preferred_element_type=jnp.float32,
    )
    member = (own_request[:, None] == jnp.arange(requests, dtype=jnp.int32)[None, :]).astype(
        jnp.float32
    )
    token_mod = jnp.dot(member, modulation, precision=lax.Precision.HIGHEST)
    mod_shift = token_mod[:, :width]
    mod_scale = token_mod[:, width : 2 * width]
    mod_gate = token_mod[:, 2 * width :]
    row_mean = jnp.mean(stream, axis=1, keepdims=True)
    centered = stream - row_mean
    row_var = jnp.mean(centered * centered, axis=1, keepdims=True)
    normed = centered * lax.rsqrt(row_var + 1e-06)
    modin = ((1.0 + mod_scale) * normed + mod_shift).astype(jnp.bfloat16)
    qkv_width = w_qkv.shape[1]
    shard_rows = gather_blk(modin)
    qkv_part = jnp.dot(shard_rows, w_qkv, preferred_element_type=jnp.float32).astype(jnp.bfloat16)
    mlp_part = jax.nn.gelu(
        jnp.dot(shard_rows, w_mlp_in, preferred_element_type=jnp.float32), approximate=True
    ).astype(jnp.bfloat16)
    joined = jnp.concatenate([qkv_part, mlp_part], axis=1)
    qkv_cols = joined[:, :qkv_width]
    mlp_act = joined[:, qkv_width:]
    heads_in = lax.all_to_all(
        lax.all_to_all(qkv_cols, BLK, split_axis=0, concat_axis=1, tiled=True),
        SEQ,
        split_axis=1,
        concat_axis=0,
        tiled=True,
    )
    query_rows = heads_in.shape[0]
    heads4 = heads_in.reshape(query_rows, local_heads, 3, head_size)
    query_ids = spread_rows(
        blk_at * query_rows + jnp.arange(query_rows, dtype=jnp.int32),
        query_rows,
        block_rows,
        tok_seq,
    )
    query_request = segment_of(query_ids, request_ends)
    angles = angles_of(jnp.take(positions, query_ids, axis=0), rope_table(head_size))
    query_rot = rotate(rms_scale(heads4[:, :, 0].astype(jnp.float32), q_gain), angles).astype(
        jnp.bfloat16
    )
    key_rot = rotate(rms_scale(heads4[:, :, 1].astype(jnp.float32), k_gain), angles).astype(
        jnp.bfloat16
    )
    value_rows = heads4[:, :, 2]
    run_top = jnp.full((query_rows, local_heads), -1e30, jnp.float32)
    kv_rows = jnp.concatenate(
        [key_rot.reshape(query_rows, -1), value_rows.reshape(query_rows, -1)], axis=1
    )
    kv_all = gather_blk(kv_rows)
    kv_half = kv_all.shape[1] // 2
    key_part = kv_all[:, :kv_half].reshape(-1, local_heads, head_size)
    value_part = kv_all[:, kv_half:].reshape(-1, local_heads, head_size)
    key_ids = spread_rows(
        jnp.arange(key_part.shape[0], dtype=jnp.int32), query_rows, block_rows, tok_seq
    )
    key_request = segment_of(key_ids, request_ends)
    kept = jnp.take(key_keep, key_ids) == 1
    visible = (
        (query_request[:, None] == key_request[None, :])
        & (kept[None, :] | (query_ids[:, None] == key_ids[None, :]))
    )[:, None, :]
    scores = (
        jnp.einsum("qhd,khd->qhk", query_rot, key_part, preferred_element_type=jnp.float32)
        * inv_root
    )
    row_high = jnp.max(jnp.where(visible, scores, -1e30), axis=2)
    new_top = jnp.maximum(run_top, row_high)
    weights = jnp.where(visible, jnp.exp(scores - new_top[:, :, None]), 0.0)
    run_norm = jnp.sum(weights, axis=2)
    run_sum = jnp.einsum(
        "qhk,khd->qhd", weights.astype(jnp.bfloat16), value_part, preferred_element_type=jnp.float32
    )
    run_top, run_norm, run_sum = (new_top, run_norm, run_sum)
    attended = (run_sum / run_norm[:, :, None]).astype(jnp.bfloat16)
    attended = attended.reshape(query_rows, local_heads * head_size)
    attn_local = lax.all_to_all(
        lax.all_to_all(attended, SEQ, split_axis=0, concat_axis=1, tiled=True),
        BLK,
        split_axis=1,
        concat_axis=0,
        tiled=True,
    )
    mlp_part = mlp_act
    partial = (
        jnp.dot(attn_local, w_attn_out, preferred_element_type=jnp.float32)
        + jnp.dot(mlp_part, w_mlp_out, preferred_element_type=jnp.float32)
    ).astype(jnp.bfloat16)
    summed = reduce_blk(partial)
    return stream + mod_gate * summed


def solution(mesh):
    zl = mesh.shape["seq"] // 2
    ys, xs = 4, mesh.shape["blk"] // 8
    fine = jax.sharding.Mesh(mesh.devices.reshape(zl, 2, ys, 2, xs), SEQ + BLK)
    in_specs = (
        P(SEQ + BLK, None),
        P(),
        P(),
        P(),
        P(),
        P(),
        P(None, BLK),
        P(None, BLK),
        P(),
        P(),
        P(BLK, None),
        P(BLK, None),
    )
    out_specs = P(SEQ + BLK, None)
    return jax.shard_map(body, mesh=fine, in_specs=in_specs, out_specs=out_specs, check_vma=False)
```

```python
import math

import jax
import jax.numpy as jnp
from jax import lax
from jax.sharding import PartitionSpec as P


def rope_table(head_size):
    first_count = head_size // 16
    second = 7 * head_size // 32
    pair_ids = jnp.arange(head_size // 2, dtype=jnp.int32)
    pair_axis = jnp.where(
        pair_ids < first_count, 0, jnp.where(pair_ids < first_count + second, 1, 2)
    )
    pair_local = jnp.where(
        pair_ids < first_count,
        pair_ids,
        jnp.where(
            pair_ids < first_count + second, pair_ids - first_count, pair_ids - first_count - second
        ),
    )
    axis_dims = jnp.where(pair_axis == 0, 2 * first_count, 2 * second)
    frequency = jnp.power(
        jnp.float32(10000.0), -(2 * pair_local).astype(jnp.float32) / axis_dims.astype(jnp.float32)
    )
    return jnp.where(
        jnp.arange(3)[:, None] == pair_axis[None, :], frequency[None, :], jnp.float32(0.0)
    )


def angles_of(places, freq_table):
    return jnp.sum(places.astype(jnp.float32)[:, :, None] * freq_table[None, :, :], axis=1)


def rotate(values, angles):
    paired = values.reshape(values.shape[:-1] + (values.shape[-1] // 2, 2))
    even_part = paired[..., 0]
    odd_part = paired[..., 1]
    cos_part = jnp.cos(angles)[:, None, :]
    sin_part = jnp.sin(angles)[:, None, :]
    turned = jnp.stack(
        [cos_part * even_part - sin_part * odd_part, sin_part * even_part + cos_part * odd_part],
        axis=-1,
    )
    return turned.reshape(values.shape)


def rms_scale(values, gain_vec):
    return values * lax.rsqrt(jnp.mean(values * values, axis=-1, keepdims=True) + 1e-06) * gain_vec


def segment_of(row_ids, request_ends):
    return jnp.sum((row_ids[:, None] >= request_ends[None, :]).astype(jnp.int32), axis=1)


def spread_rows(row_ids, query_rows, block_rows, tok_seq):
    owner = row_ids // query_rows
    within = row_ids % query_rows
    return within // block_rows * tok_seq + owner * block_rows + within % block_rows


SEQ = ("zl", "core")
BLK = ("y", "zh", "x")
PLANE = ("y", "x")
SWAP = [(0, 1), (1, 0)]


def by_half(mine, other):
    first = lax.axis_index("zh") == 0
    return jnp.where(first, mine, other), jnp.where(first, other, mine)


def gather_plane(x):
    low, high = by_half(x, lax.ppermute(x, "zh", SWAP))
    pair = jnp.stack([low, high])
    plane = lax.axis_size("y") * lax.axis_size("x")
    got = lax.all_to_all(jnp.broadcast_to(pair[None], (plane,) + pair.shape), PLANE, 0, 0, tiled=True)
    return got.reshape((lax.axis_size("y"), lax.axis_size("x"), 2) + x.shape)


def reduce_blk(y):
    plane = lax.axis_size("y") * lax.axis_size("x")
    pieces = y.reshape((plane, 2, y.shape[0] // (plane * 2)) + y.shape[1:])
    got = lax.all_to_all(pieces, PLANE, 0, 0, tiled=True)
    part = jnp.sum(got.astype(jnp.float32), axis=0)
    mine, theirs = by_half(part[0], part[1])
    return mine + lax.ppermute(theirs, "zh", SWAP)


def body(
    stream,
    key_keep,
    positions,
    lengths,
    step_index,
    mod_table,
    w_qkv,
    w_mlp_in,
    q_gain,
    k_gain,
    w_attn_out,
    w_mlp_out,
):
    blk_count = lax.axis_size(BLK)
    seq_count = lax.axis_size(SEQ)
    seq_at = lax.axis_index(SEQ)
    blk_at = lax.axis_index(BLK)
    block_rows = stream.shape[0]
    width = stream.shape[1]
    tok_seq = block_rows * blk_count
    head_size = q_gain.shape[0]
    local_heads = width // head_size // seq_count
    requests = mod_table.shape[0]
    step_total = mod_table.shape[1]
    inv_root = 1.0 / math.sqrt(head_size)
    request_ends = jnp.cumsum(lengths)
    own_rows = seq_at * tok_seq + blk_at * block_rows + jnp.arange(block_rows, dtype=jnp.int32)
    own_request = segment_of(own_rows, request_ends)
    step_pick = (jnp.arange(step_total, dtype=jnp.int32)[None, :] == step_index[:, None]).astype(
        jnp.bfloat16
    )
    modulation = jnp.einsum(
        "rs,rsk->rk",
        step_pick,
        mod_table.reshape(requests, step_total, 3 * width),
        preferred_element_type=jnp.float32,
    )
    member = (own_request[:, None] == jnp.arange(requests, dtype=jnp.int32)[None, :]).astype(
        jnp.float32
    )
    token_mod = jnp.dot(member, modulation, precision=lax.Precision.HIGHEST)
    mod_shift = token_mod[:, :width]
    mod_scale = token_mod[:, width : 2 * width]
    mod_gate = token_mod[:, 2 * width :]
    row_mean = jnp.mean(stream, axis=1, keepdims=True)
    centered = stream - row_mean
    row_var = jnp.mean(centered * centered, axis=1, keepdims=True)
    normed = centered * lax.rsqrt(row_var + 1e-06)
    modin = ((1.0 + mod_scale) * normed + mod_shift).astype(jnp.bfloat16)
    qkv_width = w_qkv.shape[1]
    shard_rows = gather_plane(modin).reshape(blk_count * block_rows, width)
    qkv_part = jnp.dot(shard_rows, w_qkv, preferred_element_type=jnp.float32).astype(jnp.bfloat16)
    mlp_part = jax.nn.gelu(
        jnp.dot(shard_rows, w_mlp_in, preferred_element_type=jnp.float32), approximate=True
    ).astype(jnp.bfloat16)
    joined = jnp.concatenate([qkv_part, mlp_part], axis=1)
    qkv_cols = joined[:, :qkv_width]
    mlp_act = joined[:, qkv_width:]
    ys, xs = lax.axis_size("y"), lax.axis_size("x")
    by_token = lax.all_to_all(qkv_cols, ("y", "x", "zh"), split_axis=0, concat_axis=1, tiled=True)
    by_token = by_token.reshape(block_rows, ys, xs, 2, -1).swapaxes(2, 3).reshape(block_rows, -1)
    heads_in = lax.all_to_all(by_token, SEQ, split_axis=1, concat_axis=0, tiled=True)
    query_rows = heads_in.shape[0]
    heads4 = heads_in.reshape(query_rows, local_heads, 3, head_size)
    query_ids = spread_rows(
        blk_at * query_rows + jnp.arange(query_rows, dtype=jnp.int32),
        query_rows,
        block_rows,
        tok_seq,
    )
    query_request = segment_of(query_ids, request_ends)
    query_places = lax.dynamic_index_in_dim(
        positions.reshape(seq_count, blk_count, block_rows, -1), blk_at, axis=1, keepdims=False
    ).reshape(query_rows, -1)
    angles = angles_of(query_places, rope_table(head_size))
    query_rot = rotate(rms_scale(heads4[:, :, 0].astype(jnp.float32), q_gain), angles).astype(
        jnp.bfloat16
    )
    key_rot = rotate(rms_scale(heads4[:, :, 1].astype(jnp.float32), k_gain), angles).astype(
        jnp.bfloat16
    )
    value_rows = heads4[:, :, 2]
    run_top = jnp.full((query_rows, local_heads), -1e30, jnp.float32)
    kv_rows = jnp.concatenate(
        [key_rot.reshape(query_rows, -1), value_rows.reshape(query_rows, -1)], axis=1
    )
    kv_all = gather_plane(kv_rows).reshape(ys, xs, 2, query_rows, 2 * local_heads, head_size)
    kv_all = kv_all.transpose(4, 0, 2, 1, 3, 5).reshape(2 * local_heads, -1, head_size)
    key_part = kv_all[:local_heads]
    value_part = kv_all[local_heads:]
    key_ids = spread_rows(
        jnp.arange(key_part.shape[1], dtype=jnp.int32), query_rows, block_rows, tok_seq
    )
    key_request = segment_of(key_ids, request_ends)
    kept = key_keep.reshape(seq_count, blk_count, block_rows).swapaxes(0, 1).reshape(-1) == 1
    visible = (
        (query_request[:, None] == key_request[None, :])
        & (kept[None, :] | (query_ids[:, None] == key_ids[None, :]))
    )[:, None, :]
    scores = (
        jnp.einsum("qhd,hkd->qhk", query_rot, key_part, preferred_element_type=jnp.float32)
        * inv_root
    )
    row_high = jnp.max(jnp.where(visible, scores, -1e30), axis=2)
    new_top = jnp.maximum(run_top, row_high)
    weights = jnp.where(visible, jnp.exp(scores - new_top[:, :, None]), 0.0)
    run_norm = jnp.sum(weights, axis=2)
    run_sum = jnp.einsum(
        "qhk,hkd->qhd", weights.astype(jnp.bfloat16), value_part, preferred_element_type=jnp.float32
    )
    run_top, run_norm, run_sum = (new_top, run_norm, run_sum)
    attended = (run_sum / run_norm[:, :, None]).astype(jnp.bfloat16)
    attended = attended.reshape(query_rows, local_heads * head_size)
    attn_feats = lax.all_to_all(attended, SEQ, split_axis=0, concat_axis=1, tiled=True)
    attn_feats = attn_feats.reshape(block_rows, ys, 2, xs, -1).swapaxes(2, 3).reshape(block_rows, -1)
    attn_local = lax.all_to_all(attn_feats, ("y", "x", "zh"), split_axis=1, concat_axis=0, tiled=True)
    mlp_out = lax.optimization_barrier(
        jnp.dot(mlp_act, w_mlp_out, preferred_element_type=jnp.float32)
    )
    partial = (jnp.dot(attn_local, w_attn_out, preferred_element_type=jnp.float32) + mlp_out).astype(
        jnp.bfloat16
    )
    summed = reduce_blk(partial)
    return stream + mod_gate * summed


def solution(mesh):
    zl = mesh.shape["seq"] // 2
    ys, xs = 4, mesh.shape["blk"] // 8
    fine = jax.sharding.Mesh(mesh.devices.reshape(zl, 2, ys, 2, xs), SEQ + BLK)
    in_specs = (
        P(SEQ + BLK, None),
        P(),
        P(),
        P(),
        P(),
        P(),
        P(None, BLK),
        P(None, BLK),
        P(),
        P(),
        P(BLK, None),
        P(BLK, None),
    )
    out_specs = P(SEQ + BLK, None)
    return jax.shard_map(body, mesh=fine, in_specs=in_specs, out_specs=out_specs, check_vma=False)
```

```python
import math

import jax
import jax.numpy as jnp
from jax import lax
from jax.sharding import PartitionSpec as P


def rope_table(head_size):
    first_count = head_size // 16
    second = 7 * head_size // 32
    pair_ids = jnp.arange(head_size // 2, dtype=jnp.int32)
    pair_axis = jnp.where(
        pair_ids < first_count, 0, jnp.where(pair_ids < first_count + second, 1, 2)
    )
    pair_local = jnp.where(
        pair_ids < first_count,
        pair_ids,
        jnp.where(
            pair_ids < first_count + second, pair_ids - first_count, pair_ids - first_count - second
        ),
    )
    axis_dims = jnp.where(pair_axis == 0, 2 * first_count, 2 * second)
    frequency = jnp.power(
        jnp.float32(10000.0), -(2 * pair_local).astype(jnp.float32) / axis_dims.astype(jnp.float32)
    )
    return jnp.where(
        jnp.arange(3)[:, None] == pair_axis[None, :], frequency[None, :], jnp.float32(0.0)
    )


def angles_of(places, freq_table):
    return jnp.sum(places.astype(jnp.float32)[:, :, None] * freq_table[None, :, :], axis=1)


def rotate(values, angles):
    paired = values.reshape(values.shape[:-1] + (values.shape[-1] // 2, 2))
    even_part = paired[..., 0]
    odd_part = paired[..., 1]
    cos_part = jnp.cos(angles)[:, None, :]
    sin_part = jnp.sin(angles)[:, None, :]
    turned = jnp.stack(
        [cos_part * even_part - sin_part * odd_part, sin_part * even_part + cos_part * odd_part],
        axis=-1,
    )
    return turned.reshape(values.shape)


def rms_scale(values, gain_vec):
    return values * lax.rsqrt(jnp.mean(values * values, axis=-1, keepdims=True) + 1e-06) * gain_vec


def segment_of(row_ids, request_ends):
    return jnp.sum((row_ids[:, None] >= request_ends[None, :]).astype(jnp.int32), axis=1)


def spread_rows(row_ids, query_rows, block_rows, tok_seq):
    owner = row_ids // query_rows
    within = row_ids % query_rows
    return within // block_rows * tok_seq + owner * block_rows + within % block_rows


SEQ = ("zl", "core")
BLK = ("y", "zh", "x")
PLANE = ("y", "x")
SWAP = [(0, 1), (1, 0)]


def by_half(mine, other):
    first = lax.axis_index("zh") == 0
    return jnp.where(first, mine, other), jnp.where(first, other, mine)


def gather_plane(x):
    low, high = by_half(x, lax.ppermute(x, "zh", SWAP))
    pair = jnp.stack([low, high])
    plane = lax.axis_size("y") * lax.axis_size("x")
    got = lax.all_to_all(jnp.broadcast_to(pair[None], (plane,) + pair.shape), PLANE, 0, 0, tiled=True)
    return got.reshape((lax.axis_size("y"), lax.axis_size("x"), 2) + x.shape)


def reduce_blk(y):
    plane = lax.axis_size("y") * lax.axis_size("x")
    pieces = y.reshape((plane, 2, y.shape[0] // (plane * 2)) + y.shape[1:])
    got = lax.all_to_all(pieces, PLANE, 0, 0, tiled=True)
    part = jnp.sum(got.astype(jnp.float32), axis=0)
    mine, theirs = by_half(part[0], part[1])
    return mine + lax.ppermute(theirs, "zh", SWAP)


def body(
    stream,
    key_keep,
    positions,
    lengths,
    step_index,
    mod_table,
    w_qkv,
    w_mlp_in,
    q_gain,
    k_gain,
    w_attn_out,
    w_mlp_out,
):
    blk_count = lax.axis_size(BLK)
    seq_count = lax.axis_size(SEQ)
    seq_at = lax.axis_index(SEQ)
    blk_at = lax.axis_index(BLK)
    block_rows = stream.shape[0]
    width = stream.shape[1]
    tok_seq = block_rows * blk_count
    head_size = q_gain.shape[0]
    local_heads = width // head_size // seq_count
    requests = mod_table.shape[0]
    step_total = mod_table.shape[1]
    inv_root = 1.0 / math.sqrt(head_size)
    request_ends = jnp.cumsum(lengths)
    own_rows = seq_at * tok_seq + blk_at * block_rows + jnp.arange(block_rows, dtype=jnp.int32)
    own_request = segment_of(own_rows, request_ends)
    step_pick = (jnp.arange(step_total, dtype=jnp.int32)[None, :] == step_index[:, None]).astype(
        jnp.bfloat16
    )
    modulation = jnp.einsum(
        "rs,rsk->rk",
        step_pick,
        mod_table.reshape(requests, step_total, 3 * width),
        preferred_element_type=jnp.float32,
    )
    member = (own_request[:, None] == jnp.arange(requests, dtype=jnp.int32)[None, :]).astype(
        jnp.float32
    )
    token_mod = jnp.dot(member, modulation, precision=lax.Precision.HIGHEST)
    mod_shift = token_mod[:, :width]
    mod_scale = token_mod[:, width : 2 * width]
    mod_gate = token_mod[:, 2 * width :]
    row_mean = jnp.mean(stream, axis=1, keepdims=True)
    centered = stream - row_mean
    row_var = jnp.mean(centered * centered, axis=1, keepdims=True)
    normed = centered * lax.rsqrt(row_var + 1e-06)
    modin = ((1.0 + mod_scale) * normed + mod_shift).astype(jnp.bfloat16)
    qkv_width = w_qkv.shape[1]
    shard_rows = gather_plane(modin).reshape(blk_count * block_rows, width)
    qkv_part = jnp.dot(shard_rows, w_qkv, preferred_element_type=jnp.float32).astype(jnp.bfloat16)
    mlp_part = jax.nn.gelu(
        jnp.dot(shard_rows, w_mlp_in, preferred_element_type=jnp.float32), approximate=True
    ).astype(jnp.bfloat16)
    joined = jnp.concatenate([qkv_part, mlp_part], axis=1)
    qkv_cols = joined[:, :qkv_width]
    mlp_act = joined[:, qkv_width:]
    ys, xs = lax.axis_size("y"), lax.axis_size("x")
    by_token = lax.all_to_all(qkv_cols, ("y", "x", "zh"), split_axis=0, concat_axis=1, tiled=True)
    by_token = by_token.reshape(block_rows, ys, xs, 2, -1).swapaxes(2, 3).reshape(block_rows, -1)
    heads_in = lax.all_to_all(by_token, SEQ, split_axis=1, concat_axis=0, tiled=True)
    query_rows = heads_in.shape[0]
    heads4 = heads_in.reshape(query_rows, local_heads, 3, head_size)
    query_ids = spread_rows(
        blk_at * query_rows + jnp.arange(query_rows, dtype=jnp.int32),
        query_rows,
        block_rows,
        tok_seq,
    )
    query_request = segment_of(query_ids, request_ends)
    query_places = lax.dynamic_index_in_dim(
        positions.reshape(seq_count, blk_count, block_rows, -1), blk_at, axis=1, keepdims=False
    ).reshape(query_rows, -1)
    angles = angles_of(query_places, rope_table(head_size))
    query_rot = rotate(rms_scale(heads4[:, :, 0].astype(jnp.float32), q_gain), angles).astype(
        jnp.bfloat16
    )
    key_rot = rotate(rms_scale(heads4[:, :, 1].astype(jnp.float32), k_gain), angles).astype(
        jnp.bfloat16
    )
    value_rows = heads4[:, :, 2]
    kv_rows = jnp.concatenate([key_rot, value_rows], axis=2)
    low, high = by_half(kv_rows, lax.ppermute(kv_rows, "zh", SWAP))
    kv_pair = jnp.stack([low, high])
    key_rank = jnp.arange(seq_count * tok_seq, dtype=jnp.int32)
    key_y = key_rank // (xs * 2 * query_rows)
    key_x = key_rank // (2 * query_rows) % xs
    key_zh = key_rank // query_rows % 2
    key_owner = (key_y * 2 + key_zh) * xs + key_x
    key_ids = key_rank // block_rows % seq_count * tok_seq + key_owner * block_rows + key_rank % block_rows
    key_request = segment_of(key_ids, request_ends)
    kept = key_keep.reshape(seq_count, ys, 2, xs, block_rows).transpose(1, 3, 2, 0, 4).reshape(-1) == 1
    visible = (query_request[:, None] == key_request[None, :]) & (
        kept[None, :] | (query_ids[:, None] == key_ids[None, :])
    )
    head_out = []
    for head in range(local_heads):
        piece = kv_pair[:, :, head]
        got = lax.all_to_all(
            jnp.broadcast_to(piece[None], (ys * xs,) + piece.shape), PLANE, 0, 0, tiled=True
        ).reshape(-1, 2 * head_size)
        key_h = got[:, :head_size]
        value_h = got[:, head_size:]
        scores = (
            jnp.einsum("qd,kd->qk", query_rot[:, head], key_h, preferred_element_type=jnp.float32)
            * inv_root
        )
        row_high = jnp.max(jnp.where(visible, scores, -1e30), axis=1)
        weights = jnp.where(visible, jnp.exp(scores - row_high[:, None]), 0.0)
        totals = jnp.sum(weights, axis=1)
        mixed = jnp.dot(weights.astype(jnp.bfloat16), value_h, preferred_element_type=jnp.float32)
        head_out.append((mixed / totals[:, None]).astype(jnp.bfloat16))
    attended = jnp.stack(head_out, axis=1)
    attended = attended.reshape(query_rows, local_heads * head_size)
    attn_feats = lax.all_to_all(attended, SEQ, split_axis=0, concat_axis=1, tiled=True)
    attn_feats = attn_feats.reshape(block_rows, ys, 2, xs, -1).swapaxes(2, 3).reshape(block_rows, -1)
    attn_local = lax.all_to_all(attn_feats, ("y", "x", "zh"), split_axis=1, concat_axis=0, tiled=True)
    mlp_out = lax.optimization_barrier(
        jnp.dot(mlp_act, w_mlp_out, preferred_element_type=jnp.float32)
    )
    partial = (jnp.dot(attn_local, w_attn_out, preferred_element_type=jnp.float32) + mlp_out).astype(
        jnp.bfloat16
    )
    summed = reduce_blk(partial)
    return stream + mod_gate * summed


def solution(mesh):
    zl = mesh.shape["seq"] // 2
    ys, xs = 4, mesh.shape["blk"] // 8
    fine = jax.sharding.Mesh(mesh.devices.reshape(zl, 2, ys, 2, xs), SEQ + BLK)
    in_specs = (
        P(SEQ + BLK, None),
        P(),
        P(),
        P(),
        P(),
        P(),
        P(None, BLK),
        P(None, BLK),
        P(),
        P(),
        P(BLK, None),
        P(BLK, None),
    )
    out_specs = P(SEQ + BLK, None)
    return jax.shard_map(body, mesh=fine, in_specs=in_specs, out_specs=out_specs, check_vma=False)
```

```python
import math

import jax
import jax.numpy as jnp
from jax import lax
from jax.sharding import PartitionSpec as P


def rope_table(head_size):
    first_count = head_size // 16
    second = 7 * head_size // 32
    pair_ids = jnp.arange(head_size // 2, dtype=jnp.int32)
    pair_axis = jnp.where(
        pair_ids < first_count, 0, jnp.where(pair_ids < first_count + second, 1, 2)
    )
    pair_local = jnp.where(
        pair_ids < first_count,
        pair_ids,
        jnp.where(
            pair_ids < first_count + second, pair_ids - first_count, pair_ids - first_count - second
        ),
    )
    axis_dims = jnp.where(pair_axis == 0, 2 * first_count, 2 * second)
    frequency = jnp.power(
        jnp.float32(10000.0), -(2 * pair_local).astype(jnp.float32) / axis_dims.astype(jnp.float32)
    )
    return jnp.where(
        jnp.arange(3)[:, None] == pair_axis[None, :], frequency[None, :], jnp.float32(0.0)
    )


def angles_of(places, freq_table):
    return jnp.sum(places.astype(jnp.float32)[:, :, None] * freq_table[None, :, :], axis=1)


def rotate(values, angles):
    paired = values.reshape(values.shape[:-1] + (values.shape[-1] // 2, 2))
    even_part = paired[..., 0]
    odd_part = paired[..., 1]
    cos_part = jnp.cos(angles)[:, None, :]
    sin_part = jnp.sin(angles)[:, None, :]
    turned = jnp.stack(
        [cos_part * even_part - sin_part * odd_part, sin_part * even_part + cos_part * odd_part],
        axis=-1,
    )
    return turned.reshape(values.shape)


def rms_scale(values, gain_vec):
    return values * lax.rsqrt(jnp.mean(values * values, axis=-1, keepdims=True) + 1e-06) * gain_vec


def segment_of(row_ids, request_ends):
    return jnp.sum((row_ids[:, None] >= request_ends[None, :]).astype(jnp.int32), axis=1)


def spread_rows(row_ids, query_rows, block_rows, tok_seq):
    owner = row_ids // query_rows
    within = row_ids % query_rows
    return within // block_rows * tok_seq + owner * block_rows + within % block_rows


SEQ = ("zl", "core")
BLK = ("y", "zh", "x")
PLANE = ("y", "x")
SWAP = [(0, 1), (1, 0)]


def by_half(mine, other):
    first = lax.axis_index("zh") == 0
    return jnp.where(first, mine, other), jnp.where(first, other, mine)


def gather_plane(low, high):
    pair = jnp.stack([low, high])
    plane = lax.axis_size("y") * lax.axis_size("x")
    got = lax.all_to_all(jnp.broadcast_to(pair[None], (plane,) + pair.shape), PLANE, 0, 0, tiled=True)
    return got.reshape((lax.axis_size("y"), lax.axis_size("x"), 2) + low.shape)


def reduce_blk(y):
    plane = lax.axis_size("y") * lax.axis_size("x")
    pieces = y.reshape((plane, 2, y.shape[0] // (plane * 2)) + y.shape[1:])
    got = lax.all_to_all(pieces, PLANE, 0, 0, tiled=True)
    part = jnp.sum(got.astype(jnp.float32), axis=0)
    mine, theirs = by_half(part[0], part[1])
    return mine + lax.ppermute(theirs, "zh", SWAP)


def body(
    stream,
    key_keep,
    positions,
    lengths,
    step_index,
    mod_table,
    w_qkv,
    w_mlp_in,
    q_gain,
    k_gain,
    w_attn_out,
    w_mlp_out,
):
    blk_count = lax.axis_size(BLK)
    seq_count = lax.axis_size(SEQ)
    seq_at = lax.axis_index(SEQ)
    blk_at = lax.axis_index(BLK)
    block_rows = stream.shape[0]
    width = stream.shape[1]
    tok_seq = block_rows * blk_count
    head_size = q_gain.shape[0]
    local_heads = width // head_size // seq_count
    requests = mod_table.shape[0]
    step_total = mod_table.shape[1]
    inv_root = 1.0 / math.sqrt(head_size)
    request_ends = jnp.cumsum(lengths)
    partner_blk = blk_at + lax.axis_size("x") * (1 - 2 * lax.axis_index("zh"))
    partner_stream = lax.ppermute(stream, "zh", SWAP)
    step_pick = (jnp.arange(step_total, dtype=jnp.int32)[None, :] == step_index[:, None]).astype(
        jnp.bfloat16
    )
    modulation = jnp.einsum(
        "rs,rsk->rk",
        step_pick,
        mod_table.reshape(requests, step_total, 3 * width),
        preferred_element_type=jnp.float32,
    )

    def modulated(rows, row_blk):
        row_ids = seq_at * tok_seq + row_blk * block_rows + jnp.arange(block_rows, dtype=jnp.int32)
        row_request = segment_of(row_ids, request_ends)
        member = (row_request[:, None] == jnp.arange(requests, dtype=jnp.int32)[None, :]).astype(
            jnp.float32
        )
        token_mod = jnp.dot(member, modulation, precision=lax.Precision.HIGHEST)
        mod_shift = token_mod[:, :width]
        mod_scale = token_mod[:, width : 2 * width]
        row_mean = jnp.mean(rows, axis=1, keepdims=True)
        centered = rows - row_mean
        row_var = jnp.mean(centered * centered, axis=1, keepdims=True)
        normed = centered * lax.rsqrt(row_var + 1e-06)
        return ((1.0 + mod_scale) * normed + mod_shift).astype(jnp.bfloat16), token_mod[:, 2 * width :]

    modin, mod_gate = modulated(stream, blk_at)
    partner_modin, _ = modulated(partner_stream, partner_blk)
    qkv_width = w_qkv.shape[1]
    shard_rows = gather_plane(*by_half(modin, partner_modin)).reshape(blk_count * block_rows, width)
    qkv_part = jnp.dot(shard_rows, w_qkv, preferred_element_type=jnp.float32).astype(jnp.bfloat16)
    mlp_part = jax.nn.gelu(
        jnp.dot(shard_rows, w_mlp_in, preferred_element_type=jnp.float32), approximate=True
    ).astype(jnp.bfloat16)
    joined = jnp.concatenate([qkv_part, mlp_part], axis=1)
    qkv_cols = joined[:, :qkv_width]
    mlp_act = joined[:, qkv_width:]
    ys, xs = lax.axis_size("y"), lax.axis_size("x")
    by_token = lax.all_to_all(qkv_cols, ("y", "x", "zh"), split_axis=0, concat_axis=1, tiled=True)
    by_token = by_token.reshape(block_rows, ys, xs, 2, -1).swapaxes(2, 3).reshape(block_rows, -1)
    heads_in = lax.all_to_all(by_token, SEQ, split_axis=1, concat_axis=0, tiled=True)
    query_rows = heads_in.shape[0]
    heads4 = heads_in.reshape(query_rows, local_heads, 3, head_size)
    query_ids = spread_rows(
        blk_at * query_rows + jnp.arange(query_rows, dtype=jnp.int32),
        query_rows,
        block_rows,
        tok_seq,
    )
    query_request = segment_of(query_ids, request_ends)
    query_places = lax.dynamic_index_in_dim(
        positions.reshape(seq_count, blk_count, block_rows, -1), blk_at, axis=1, keepdims=False
    ).reshape(query_rows, -1)
    angles = angles_of(query_places, rope_table(head_size))
    query_rot = rotate(rms_scale(heads4[:, :, 0].astype(jnp.float32), q_gain), angles).astype(
        jnp.bfloat16
    )
    key_rot = rotate(rms_scale(heads4[:, :, 1].astype(jnp.float32), k_gain), angles).astype(
        jnp.bfloat16
    )
    value_rows = heads4[:, :, 2]
    kv_rows = jnp.concatenate([key_rot, value_rows], axis=2)
    partner_raw = lax.ppermute(heads4[:, :, 1:], "zh", SWAP)
    partner_places = lax.dynamic_index_in_dim(
        positions.reshape(seq_count, blk_count, block_rows, -1), partner_blk, axis=1, keepdims=False
    ).reshape(query_rows, -1)
    partner_key = rotate(
        rms_scale(partner_raw[:, :, 0].astype(jnp.float32), k_gain),
        angles_of(partner_places, rope_table(head_size)),
    ).astype(jnp.bfloat16)
    partner_rows = jnp.concatenate([partner_key, partner_raw[:, :, 1]], axis=2)
    kv_pair = jnp.stack(by_half(kv_rows, partner_rows))
    key_rank = jnp.arange(seq_count * tok_seq, dtype=jnp.int32)
    key_y = key_rank // (xs * 2 * query_rows)
    key_x = key_rank // (2 * query_rows) % xs
    key_zh = key_rank // query_rows % 2
    key_owner = (key_y * 2 + key_zh) * xs + key_x
    key_ids = key_rank // block_rows % seq_count * tok_seq + key_owner * block_rows + key_rank % block_rows
    key_request = segment_of(key_ids, request_ends)
    kept = key_keep.reshape(seq_count, ys, 2, xs, block_rows).transpose(1, 3, 2, 0, 4).reshape(-1) == 1
    visible = (query_request[:, None] == key_request[None, :]) & (
        kept[None, :] | (query_ids[:, None] == key_ids[None, :])
    )
    head_out = []
    for head in range(local_heads):
        piece = kv_pair[:, :, head]
        got = lax.all_to_all(
            jnp.broadcast_to(piece[None], (ys * xs,) + piece.shape), PLANE, 0, 0, tiled=True
        ).reshape(-1, 2 * head_size)
        key_h = got[:, :head_size]
        value_h = got[:, head_size:]
        scores = (
            jnp.einsum("qd,kd->qk", query_rot[:, head], key_h, preferred_element_type=jnp.float32)
            * inv_root
        )
        row_high = jnp.max(jnp.where(visible, scores, -1e30), axis=1)
        weights = jnp.where(visible, jnp.exp(scores - row_high[:, None]), 0.0)
        totals = jnp.sum(weights, axis=1)
        mixed = jnp.dot(weights.astype(jnp.bfloat16), value_h, preferred_element_type=jnp.float32)
        head_out.append((mixed / totals[:, None]).astype(jnp.bfloat16))
    attended = jnp.stack(head_out, axis=1)
    attended = attended.reshape(query_rows, local_heads * head_size)
    attn_feats = lax.all_to_all(attended, SEQ, split_axis=0, concat_axis=1, tiled=True)
    attn_feats = attn_feats.reshape(block_rows, ys, 2, xs, -1).swapaxes(2, 3).reshape(block_rows, -1)
    attn_local = lax.all_to_all(attn_feats, ("y", "x", "zh"), split_axis=1, concat_axis=0, tiled=True)
    mlp_out = lax.optimization_barrier(
        jnp.dot(mlp_act, w_mlp_out, preferred_element_type=jnp.float32)
    )
    partial = (jnp.dot(attn_local, w_attn_out, preferred_element_type=jnp.float32) + mlp_out).astype(
        jnp.bfloat16
    )
    summed = reduce_blk(partial)
    return stream + mod_gate * summed


def solution(mesh):
    zl = mesh.shape["seq"] // 2
    ys, xs = 4, mesh.shape["blk"] // 8
    fine = jax.sharding.Mesh(mesh.devices.reshape(zl, 2, ys, 2, xs), SEQ + BLK)
    in_specs = (
        P(SEQ + BLK, None),
        P(),
        P(),
        P(),
        P(),
        P(),
        P(None, BLK),
        P(None, BLK),
        P(),
        P(),
        P(BLK, None),
        P(BLK, None),
    )
    out_specs = P(SEQ + BLK, None)
    return jax.shard_map(body, mesh=fine, in_specs=in_specs, out_specs=out_specs, check_vma=False)
```

```python
import math

import jax
import jax.numpy as jnp
from jax import lax
from jax.sharding import PartitionSpec as P


def rope_table(head_size):
    first_count = head_size // 16
    second = 7 * head_size // 32
    pair_ids = jnp.arange(head_size // 2, dtype=jnp.int32)
    pair_axis = jnp.where(
        pair_ids < first_count, 0, jnp.where(pair_ids < first_count + second, 1, 2)
    )
    pair_local = jnp.where(
        pair_ids < first_count,
        pair_ids,
        jnp.where(
            pair_ids < first_count + second, pair_ids - first_count, pair_ids - first_count - second
        ),
    )
    axis_dims = jnp.where(pair_axis == 0, 2 * first_count, 2 * second)
    frequency = jnp.power(
        jnp.float32(10000.0), -(2 * pair_local).astype(jnp.float32) / axis_dims.astype(jnp.float32)
    )
    return jnp.where(
        jnp.arange(3)[:, None] == pair_axis[None, :], frequency[None, :], jnp.float32(0.0)
    )


def angles_of(places, freq_table):
    return jnp.sum(places.astype(jnp.float32)[:, :, None] * freq_table[None, :, :], axis=1)


def rotate(values, angles):
    paired = values.reshape(values.shape[:-1] + (values.shape[-1] // 2, 2))
    even_part = paired[..., 0]
    odd_part = paired[..., 1]
    cos_part = jnp.cos(angles)[:, None, :]
    sin_part = jnp.sin(angles)[:, None, :]
    turned = jnp.stack(
        [cos_part * even_part - sin_part * odd_part, sin_part * even_part + cos_part * odd_part],
        axis=-1,
    )
    return turned.reshape(values.shape)


def rms_scale(values, gain_vec):
    return values * lax.rsqrt(jnp.mean(values * values, axis=-1, keepdims=True) + 1e-06) * gain_vec


def segment_of(row_ids, request_ends):
    return jnp.sum((row_ids[:, None] >= request_ends[None, :]).astype(jnp.int32), axis=1)


def spread_rows(row_ids, query_rows, block_rows, tok_seq):
    owner = row_ids // query_rows
    within = row_ids % query_rows
    return within // block_rows * tok_seq + owner * block_rows + within % block_rows


SEQ = ("zl", "core")
BLK = ("y", "zh", "x")
PLANE = ("y", "x")
SWAP = [(0, 1), (1, 0)]


def by_half(mine, other):
    first = lax.axis_index("zh") == 0
    return jnp.where(first, mine, other), jnp.where(first, other, mine)


def gather_plane(low, high):
    pair = jnp.stack([low, high])
    plane = lax.axis_size("y") * lax.axis_size("x")
    got = lax.all_to_all(jnp.broadcast_to(pair[None], (plane,) + pair.shape), PLANE, 0, 0, tiled=True)
    return got.reshape((lax.axis_size("y"), lax.axis_size("x"), 2) + low.shape)


def reduce_blk(y):
    plane = lax.axis_size("y") * lax.axis_size("x")
    pieces = y.reshape((plane, 2, y.shape[0] // (plane * 2)) + y.shape[1:])
    got = lax.all_to_all(pieces, PLANE, 0, 0, tiled=True)
    part = jnp.sum(got.astype(jnp.float32), axis=0)
    mine, theirs = by_half(part[0], part[1])
    return mine + lax.ppermute(theirs, "zh", SWAP)


def body(
    stream,
    key_keep,
    positions,
    lengths,
    step_index,
    mod_table,
    w_qkv,
    w_mlp_in,
    q_gain,
    k_gain,
    w_attn_out,
    w_mlp_out,
):
    blk_count = lax.axis_size(BLK)
    seq_count = lax.axis_size(SEQ)
    seq_at = lax.axis_index(SEQ)
    blk_at = lax.axis_index(BLK)
    block_rows = stream.shape[0]
    width = stream.shape[1]
    tok_seq = block_rows * blk_count
    head_size = q_gain.shape[0]
    local_heads = width // head_size // seq_count
    requests = mod_table.shape[0]
    step_total = mod_table.shape[1]
    inv_root = 1.0 / math.sqrt(head_size)
    request_ends = jnp.cumsum(lengths)
    partner_blk = blk_at + lax.axis_size("x") * (1 - 2 * lax.axis_index("zh"))
    partner_stream = lax.ppermute(stream, "zh", SWAP)
    step_pick = (jnp.arange(step_total, dtype=jnp.int32)[None, :] == step_index[:, None]).astype(
        jnp.bfloat16
    )
    modulation = jnp.einsum(
        "rs,rsk->rk",
        step_pick,
        mod_table.reshape(requests, step_total, 3 * width),
        preferred_element_type=jnp.float32,
    )

    def modulated(rows, row_blk):
        row_ids = seq_at * tok_seq + row_blk * block_rows + jnp.arange(block_rows, dtype=jnp.int32)
        row_request = segment_of(row_ids, request_ends)
        member = (row_request[:, None] == jnp.arange(requests, dtype=jnp.int32)[None, :]).astype(
            jnp.float32
        )
        token_mod = jnp.dot(member, modulation, precision=lax.Precision.HIGHEST)
        mod_shift = token_mod[:, :width]
        mod_scale = token_mod[:, width : 2 * width]
        row_mean = jnp.mean(rows, axis=1, keepdims=True)
        centered = rows - row_mean
        row_var = jnp.mean(centered * centered, axis=1, keepdims=True)
        normed = centered * lax.rsqrt(row_var + 1e-06)
        return ((1.0 + mod_scale) * normed + mod_shift).astype(jnp.bfloat16), token_mod[:, 2 * width :]

    modin, mod_gate = modulated(stream, blk_at)
    partner_modin, _ = modulated(partner_stream, partner_blk)
    qkv_width = w_qkv.shape[1]
    shard_rows = gather_plane(*by_half(modin, partner_modin)).reshape(blk_count * block_rows, width)
    qkv_part = jnp.dot(shard_rows, w_qkv, preferred_element_type=jnp.float32).astype(jnp.bfloat16)
    mlp_part = jax.nn.gelu(
        jnp.dot(shard_rows, w_mlp_in, preferred_element_type=jnp.float32), approximate=True
    ).astype(jnp.bfloat16)
    joined = jnp.concatenate([qkv_part, mlp_part], axis=1)
    qkv_cols = joined[:, :qkv_width]
    mlp_act = joined[:, qkv_width:]
    ys, xs = lax.axis_size("y"), lax.axis_size("x")
    by_token = lax.all_to_all(qkv_cols, ("y", "x", "zh"), split_axis=0, concat_axis=1, tiled=True)
    by_token = by_token.reshape(block_rows, ys, xs, 2, -1).swapaxes(2, 3).reshape(block_rows, -1)
    group = ("zl", "zh")
    heads_in = lax.all_to_all(by_token, group, split_axis=1, concat_axis=0, tiled=True)
    query_rows = heads_in.shape[0]
    heads4 = heads_in.reshape(query_rows, local_heads, 3, head_size)
    core_at, y_at, x_at = lax.axis_index("core"), lax.axis_index("y"), lax.axis_index("x")
    digits = (lax.axis_size("zl"), 2, ys, 2, xs, block_rows)
    token_grid = jnp.arange(seq_count * tok_seq, dtype=jnp.int32).reshape(digits)

    def own_queries(grid):
        grid = lax.dynamic_index_in_dim(grid, core_at, axis=1, keepdims=False)
        grid = lax.dynamic_index_in_dim(grid, y_at, axis=1, keepdims=False)
        grid = lax.dynamic_index_in_dim(grid, x_at, axis=2, keepdims=False)
        return grid.reshape((query_rows,) + grid.shape[3:])

    query_ids = own_queries(token_grid)
    query_request = segment_of(query_ids, request_ends)
    angles = angles_of(own_queries(positions.reshape(digits + (-1,))), rope_table(head_size))
    query_rot = rotate(rms_scale(heads4[:, :, 0].astype(jnp.float32), q_gain), angles).astype(
        jnp.bfloat16
    )
    key_rot = rotate(rms_scale(heads4[:, :, 1].astype(jnp.float32), k_gain), angles).astype(
        jnp.bfloat16
    )
    value_rows = heads4[:, :, 2]
    kv_rows = jnp.concatenate([key_rot, value_rows], axis=2)
    key_order = (1, 2, 4, 0, 3, 5)
    key_ids = token_grid.transpose(key_order).reshape(-1)
    key_request = segment_of(key_ids, request_ends)
    kept = key_keep.reshape(digits).transpose(key_order).reshape(-1) == 1
    visible = (query_request[:, None] == key_request[None, :]) & (
        kept[None, :] | (query_ids[:, None] == key_ids[None, :])
    )
    first_core = core_at == 0
    head_out = []
    for head in range(local_heads):
        piece = kv_rows[:, head]
        got = lax.all_to_all(
            jnp.broadcast_to(piece[None], (ys * xs,) + piece.shape), PLANE, 0, 0, tiled=True
        )
        sibling = lax.ppermute(got, "core", SWAP)
        both = jnp.stack([jnp.where(first_core, got, sibling), jnp.where(first_core, sibling, got)])
        both = both.reshape(-1, 2 * head_size)
        key_h = both[:, :head_size]
        value_h = both[:, head_size:]
        scores = (
            jnp.einsum("qd,kd->qk", query_rot[:, head], key_h, preferred_element_type=jnp.float32)
            * inv_root
        )
        row_high = jnp.max(jnp.where(visible, scores, -1e30), axis=1)
        weights = jnp.where(visible, jnp.exp(scores - row_high[:, None]), 0.0)
        totals = jnp.sum(weights, axis=1)
        mixed = jnp.dot(weights.astype(jnp.bfloat16), value_h, preferred_element_type=jnp.float32)
        head_out.append((mixed / totals[:, None]).astype(jnp.bfloat16))
    attended = jnp.stack(head_out, axis=1)
    attended = attended.reshape(query_rows, local_heads * head_size)
    attn_feats = lax.all_to_all(attended, group, split_axis=0, concat_axis=1, tiled=True)
    attn_feats = attn_feats.reshape(block_rows, ys, 2, xs, -1).swapaxes(2, 3).reshape(block_rows, -1)
    attn_local = lax.all_to_all(attn_feats, ("y", "x", "zh"), split_axis=1, concat_axis=0, tiled=True)
    mlp_out = lax.optimization_barrier(
        jnp.dot(mlp_act, w_mlp_out, preferred_element_type=jnp.float32)
    )
    partial = (jnp.dot(attn_local, w_attn_out, preferred_element_type=jnp.float32) + mlp_out).astype(
        jnp.bfloat16
    )
    summed = reduce_blk(partial)
    return stream + mod_gate * summed


def solution(mesh):
    zl = mesh.shape["seq"] // 2
    ys, xs = 4, mesh.shape["blk"] // 8
    fine = jax.sharding.Mesh(mesh.devices.reshape(zl, 2, ys, 2, xs), SEQ + BLK)
    in_specs = (
        P(SEQ + BLK, None),
        P(),
        P(),
        P(),
        P(),
        P(),
        P(None, BLK),
        P(None, BLK),
        P(),
        P(),
        P(BLK, None),
        P(BLK, None),
    )
    out_specs = P(SEQ + BLK, None)
    return jax.shard_map(body, mesh=fine, in_specs=in_specs, out_specs=out_specs, check_vma=False)
```

```python
import math

import jax
import jax.numpy as jnp
from jax import lax
from jax.sharding import PartitionSpec as P


def rope_table(head_size):
    first_count = head_size // 16
    second = 7 * head_size // 32
    pair_ids = jnp.arange(head_size // 2, dtype=jnp.int32)
    pair_axis = jnp.where(
        pair_ids < first_count, 0, jnp.where(pair_ids < first_count + second, 1, 2)
    )
    pair_local = jnp.where(
        pair_ids < first_count,
        pair_ids,
        jnp.where(
            pair_ids < first_count + second, pair_ids - first_count, pair_ids - first_count - second
        ),
    )
    axis_dims = jnp.where(pair_axis == 0, 2 * first_count, 2 * second)
    frequency = jnp.power(
        jnp.float32(10000.0), -(2 * pair_local).astype(jnp.float32) / axis_dims.astype(jnp.float32)
    )
    return jnp.where(
        jnp.arange(3)[:, None] == pair_axis[None, :], frequency[None, :], jnp.float32(0.0)
    )


def angles_of(places, freq_table):
    return jnp.sum(places.astype(jnp.float32)[:, :, None] * freq_table[None, :, :], axis=1)


def rotate(values, angles):
    paired = values.reshape(values.shape[:-1] + (values.shape[-1] // 2, 2))
    even_part = paired[..., 0]
    odd_part = paired[..., 1]
    cos_part = jnp.cos(angles)[:, None, :]
    sin_part = jnp.sin(angles)[:, None, :]
    turned = jnp.stack(
        [cos_part * even_part - sin_part * odd_part, sin_part * even_part + cos_part * odd_part],
        axis=-1,
    )
    return turned.reshape(values.shape)


def rms_scale(values, gain_vec):
    return values * lax.rsqrt(jnp.mean(values * values, axis=-1, keepdims=True) + 1e-06) * gain_vec


def segment_of(row_ids, request_ends):
    return jnp.sum((row_ids[:, None] >= request_ends[None, :]).astype(jnp.int32), axis=1)


def spread_rows(row_ids, query_rows, block_rows, tok_seq):
    owner = row_ids // query_rows
    within = row_ids % query_rows
    return within // block_rows * tok_seq + owner * block_rows + within % block_rows


SEQ = ("zl", "core")
BLK = ("y", "zh", "x")
PLANE = ("y", "x")
SWAP = [(0, 1), (1, 0)]


def by_half(mine, other):
    first = lax.axis_index("zh") == 0
    return jnp.where(first, mine, other), jnp.where(first, other, mine)


def gather_plane(low, high):
    pair = jnp.stack([low, high])
    plane = lax.axis_size("y") * lax.axis_size("x")
    got = lax.all_to_all(jnp.broadcast_to(pair[None], (plane,) + pair.shape), PLANE, 0, 0, tiled=True)
    return got.reshape((lax.axis_size("y"), lax.axis_size("x"), 2) + low.shape)


def reduce_blk(y):
    plane = lax.axis_size("y") * lax.axis_size("x")
    pieces = y.reshape((plane, 2, y.shape[0] // (plane * 2)) + y.shape[1:])
    got = lax.all_to_all(pieces, PLANE, 0, 0, tiled=True)
    part = jnp.sum(got.astype(jnp.float32), axis=0)
    mine, theirs = by_half(part[0], part[1])
    return mine + lax.ppermute(theirs, "zh", SWAP)


def body(
    stream,
    key_keep,
    positions,
    lengths,
    step_index,
    mod_table,
    w_qkv,
    w_mlp_in,
    q_gain,
    k_gain,
    w_attn_out,
    w_mlp_out,
):
    blk_count = lax.axis_size(BLK)
    seq_count = lax.axis_size(SEQ)
    seq_at = lax.axis_index(SEQ)
    blk_at = lax.axis_index(BLK)
    block_rows = stream.shape[0]
    width = stream.shape[1]
    tok_seq = block_rows * blk_count
    head_size = q_gain.shape[0]
    local_heads = width // head_size // seq_count
    requests = mod_table.shape[0]
    step_total = mod_table.shape[1]
    inv_root = 1.0 / math.sqrt(head_size)
    request_ends = jnp.cumsum(lengths)
    partner_blk = blk_at + lax.axis_size("x") * (1 - 2 * lax.axis_index("zh"))
    partner_stream = lax.ppermute(stream, "zh", SWAP)
    step_pick = (jnp.arange(step_total, dtype=jnp.int32)[None, :] == step_index[:, None]).astype(
        jnp.bfloat16
    )
    modulation = jnp.einsum(
        "rs,rsk->rk",
        step_pick,
        mod_table.reshape(requests, step_total, 3 * width),
        preferred_element_type=jnp.float32,
    )

    def modulated(rows, row_blk):
        row_ids = seq_at * tok_seq + row_blk * block_rows + jnp.arange(block_rows, dtype=jnp.int32)
        row_request = segment_of(row_ids, request_ends)
        member = (row_request[:, None] == jnp.arange(requests, dtype=jnp.int32)[None, :]).astype(
            jnp.float32
        )
        token_mod = jnp.dot(member, modulation, precision=lax.Precision.HIGHEST)
        mod_shift = token_mod[:, :width]
        mod_scale = token_mod[:, width : 2 * width]
        row_mean = jnp.mean(rows, axis=1, keepdims=True)
        centered = rows - row_mean
        row_var = jnp.mean(centered * centered, axis=1, keepdims=True)
        normed = centered * lax.rsqrt(row_var + 1e-06)
        return ((1.0 + mod_scale) * normed + mod_shift).astype(jnp.bfloat16), token_mod[:, 2 * width :]

    modin, mod_gate = modulated(stream, blk_at)
    partner_modin, _ = modulated(partner_stream, partner_blk)
    qkv_width = w_qkv.shape[1]
    shard_rows = gather_plane(*by_half(modin, partner_modin)).reshape(blk_count * block_rows, width)
    qkv_part = jnp.dot(shard_rows, w_qkv, preferred_element_type=jnp.float32).astype(jnp.bfloat16)
    mlp_part = jax.nn.gelu(
        jnp.dot(shard_rows, w_mlp_in, preferred_element_type=jnp.float32), approximate=True
    ).astype(jnp.bfloat16)
    joined = jnp.concatenate([qkv_part, mlp_part], axis=1)
    qkv_cols = joined[:, :qkv_width]
    mlp_act = joined[:, qkv_width:]
    ys, xs = lax.axis_size("y"), lax.axis_size("x")
    zl_count = lax.axis_size("zl")
    flip = [(a * ys + b, b * zl_count + a) for a in range(zl_count) for b in range(ys)]
    quarters = lax.all_to_all(qkv_cols.reshape(xs, -1, qkv_cols.shape[1]), "x", 0, 0, tiled=True)
    quarters = quarters.swapaxes(0, 1).reshape(quarters.shape[1], -1)
    heads_in = lax.ppermute(quarters, ("zl", "y"), flip)
    query_rows = heads_in.shape[0]
    heads4 = heads_in.reshape(query_rows, local_heads, 3, head_size)
    core_at, y_at, x_at = lax.axis_index("core"), lax.axis_index("y"), lax.axis_index("x")
    digits = (lax.axis_size("zl"), 2, ys, 2, xs, block_rows)
    token_grid = jnp.arange(seq_count * tok_seq, dtype=jnp.int32).reshape(digits)

    def own_queries(grid):
        grid = lax.dynamic_index_in_dim(grid, x_at, axis=2, keepdims=False)
        grid = lax.dynamic_index_in_dim(grid, core_at, axis=1, keepdims=False)
        grid = lax.dynamic_index_in_dim(grid, y_at, axis=0, keepdims=False)
        return grid.swapaxes(0, 1).reshape((query_rows,) + grid.shape[3:])

    query_ids = own_queries(token_grid)
    query_request = segment_of(query_ids, request_ends)
    angles = angles_of(own_queries(positions.reshape(digits + (-1,))), rope_table(head_size))
    query_rot = rotate(rms_scale(heads4[:, :, 0].astype(jnp.float32), q_gain), angles).astype(
        jnp.bfloat16
    )
    key_rot = rotate(rms_scale(heads4[:, :, 1].astype(jnp.float32), k_gain), angles).astype(
        jnp.bfloat16
    )
    value_rows = heads4[:, :, 2]
    kv_rows = jnp.concatenate([key_rot, value_rows], axis=2)
    key_order = (1, 0, 2, 4, 3, 5)
    key_ids = token_grid.transpose(key_order).reshape(-1)
    key_request = segment_of(key_ids, request_ends)
    kept = key_keep.reshape(digits).transpose(key_order).reshape(-1) == 1
    visible = (query_request[:, None] == key_request[None, :]) & (
        kept[None, :] | (query_ids[:, None] == key_ids[None, :])
    )
    first_core = core_at == 0
    head_out = []
    for head in range(local_heads):
        piece = kv_rows[:, head]
        got = lax.all_to_all(
            jnp.broadcast_to(piece[None], (ys * xs,) + piece.shape), PLANE, 0, 0, tiled=True
        )
        sibling = lax.ppermute(got, "core", SWAP)
        both = jnp.stack([jnp.where(first_core, got, sibling), jnp.where(first_core, sibling, got)])
        both = both.reshape(-1, 2 * head_size)
        key_h = both[:, :head_size]
        value_h = both[:, head_size:]
        scores = (
            jnp.einsum("qd,kd->qk", query_rot[:, head], key_h, preferred_element_type=jnp.float32)
            * inv_root
        )
        row_high = jnp.max(jnp.where(visible, scores, -1e30), axis=1)
        weights = jnp.where(visible, jnp.exp(scores - row_high[:, None]), 0.0)
        totals = jnp.sum(weights, axis=1)
        mixed = jnp.dot(weights.astype(jnp.bfloat16), value_h, preferred_element_type=jnp.float32)
        head_out.append((mixed / totals[:, None]).astype(jnp.bfloat16))
    attended = jnp.stack(head_out, axis=1)
    attended = attended.reshape(query_rows, local_heads * head_size)
    attn_back = lax.ppermute(attended, ("zl", "y"), flip)
    attn_local = lax.all_to_all(
        attn_back.reshape(query_rows, xs, -1), "x", 1, 0, tiled=True
    ).reshape(xs * query_rows, -1)
    mlp_out = lax.optimization_barrier(
        jnp.dot(mlp_act, w_mlp_out, preferred_element_type=jnp.float32)
    )
    partial = (jnp.dot(attn_local, w_attn_out, preferred_element_type=jnp.float32) + mlp_out).astype(
        jnp.bfloat16
    )
    summed = reduce_blk(partial)
    return stream + mod_gate * summed


def solution(mesh):
    zl = mesh.shape["seq"] // 2
    ys, xs = 4, mesh.shape["blk"] // 8
    fine = jax.sharding.Mesh(mesh.devices.reshape(zl, 2, ys, 2, xs), SEQ + BLK)
    in_specs = (
        P(SEQ + BLK, None),
        P(),
        P(),
        P(),
        P(),
        P(),
        P(None, BLK),
        P(None, BLK),
        P(),
        P(),
        P(BLK, None),
        P(BLK, None),
    )
    out_specs = P(SEQ + BLK, None)
    return jax.shard_map(body, mesh=fine, in_specs=in_specs, out_specs=out_specs, check_vma=False)
```

```python
import math

import jax
import jax.numpy as jnp
from jax import lax
from jax.sharding import PartitionSpec as P


def rope_table(head_size):
    first_count = head_size // 16
    second = 7 * head_size // 32
    pair_ids = jnp.arange(head_size // 2, dtype=jnp.int32)
    pair_axis = jnp.where(
        pair_ids < first_count, 0, jnp.where(pair_ids < first_count + second, 1, 2)
    )
    pair_local = jnp.where(
        pair_ids < first_count,
        pair_ids,
        jnp.where(
            pair_ids < first_count + second, pair_ids - first_count, pair_ids - first_count - second
        ),
    )
    axis_dims = jnp.where(pair_axis == 0, 2 * first_count, 2 * second)
    frequency = jnp.power(
        jnp.float32(10000.0), -(2 * pair_local).astype(jnp.float32) / axis_dims.astype(jnp.float32)
    )
    return jnp.where(
        jnp.arange(3)[:, None] == pair_axis[None, :], frequency[None, :], jnp.float32(0.0)
    )


def angles_of(places, freq_table):
    return jnp.sum(places.astype(jnp.float32)[:, :, None] * freq_table[None, :, :], axis=1)


def rotate(values, angles):
    paired = values.reshape(values.shape[:-1] + (values.shape[-1] // 2, 2))
    even_part = paired[..., 0]
    odd_part = paired[..., 1]
    cos_part = jnp.cos(angles)[:, None, :]
    sin_part = jnp.sin(angles)[:, None, :]
    turned = jnp.stack(
        [cos_part * even_part - sin_part * odd_part, sin_part * even_part + cos_part * odd_part],
        axis=-1,
    )
    return turned.reshape(values.shape)


def rms_scale(values, gain_vec):
    return values * lax.rsqrt(jnp.mean(values * values, axis=-1, keepdims=True) + 1e-06) * gain_vec


def segment_of(row_ids, request_ends):
    return jnp.sum((row_ids[:, None] >= request_ends[None, :]).astype(jnp.int32), axis=1)


def spread_rows(row_ids, query_rows, block_rows, tok_seq):
    owner = row_ids // query_rows
    within = row_ids % query_rows
    return within // block_rows * tok_seq + owner * block_rows + within % block_rows


SEQ = ("zl", "core")
BLK = ("y", "zh", "x")
PLANE = ("y", "x")
SWAP = [(0, 1), (1, 0)]


def by_half(mine, other):
    first = lax.axis_index("zh") == 0
    return jnp.where(first, mine, other), jnp.where(first, other, mine)


def gather_plane(low, high):
    pair = jnp.stack([low, high])
    plane = lax.axis_size("y") * lax.axis_size("x")
    got = lax.all_to_all(jnp.broadcast_to(pair[None], (plane,) + pair.shape), PLANE, 0, 0, tiled=True)
    return got.reshape((lax.axis_size("y"), lax.axis_size("x"), 2) + low.shape)


def reduce_blk(y):
    plane = lax.axis_size("y") * lax.axis_size("x")
    pieces = y.reshape((plane, 2, y.shape[0] // (plane * 2)) + y.shape[1:])
    got = lax.all_to_all(pieces, PLANE, 0, 0, tiled=True)
    part = jnp.sum(got.astype(jnp.float32), axis=0)
    mine, theirs = by_half(part[0], part[1])
    return mine + lax.ppermute(theirs, "zh", SWAP)


def body(
    stream,
    key_keep,
    positions,
    lengths,
    step_index,
    mod_table,
    w_qkv,
    w_mlp_in,
    q_gain,
    k_gain,
    w_attn_out,
    w_mlp_out,
):
    blk_count = lax.axis_size(BLK)
    seq_count = lax.axis_size(SEQ)
    seq_at = lax.axis_index(SEQ)
    blk_at = lax.axis_index(BLK)
    block_rows = stream.shape[0]
    width = stream.shape[1]
    tok_seq = block_rows * blk_count
    head_size = q_gain.shape[0]
    local_heads = width // head_size // seq_count
    requests = mod_table.shape[0]
    step_total = mod_table.shape[1]
    inv_root = 1.0 / math.sqrt(head_size)
    request_ends = jnp.cumsum(lengths)
    partner_blk = blk_at + lax.axis_size("x") * (1 - 2 * lax.axis_index("zh"))
    partner_stream = lax.ppermute(stream, "zh", SWAP)
    step_pick = (jnp.arange(step_total, dtype=jnp.int32)[None, :] == step_index[:, None]).astype(
        jnp.bfloat16
    )
    modulation = jnp.einsum(
        "rs,rsk->rk",
        step_pick,
        mod_table.reshape(requests, step_total, 3 * width),
        preferred_element_type=jnp.float32,
    )

    def modulated(rows, row_blk):
        row_ids = seq_at * tok_seq + row_blk * block_rows + jnp.arange(block_rows, dtype=jnp.int32)
        row_request = segment_of(row_ids, request_ends)
        member = (row_request[:, None] == jnp.arange(requests, dtype=jnp.int32)[None, :]).astype(
            jnp.float32
        )
        token_mod = jnp.dot(member, modulation, precision=lax.Precision.HIGHEST)
        mod_shift = token_mod[:, :width]
        mod_scale = token_mod[:, width : 2 * width]
        row_mean = jnp.mean(rows, axis=1, keepdims=True)
        centered = rows - row_mean
        row_var = jnp.mean(centered * centered, axis=1, keepdims=True)
        normed = centered * lax.rsqrt(row_var + 1e-06)
        return ((1.0 + mod_scale) * normed + mod_shift).astype(jnp.bfloat16), token_mod[:, 2 * width :]

    modin, mod_gate = modulated(stream, blk_at)
    partner_modin, _ = modulated(partner_stream, partner_blk)
    qkv_width = w_qkv.shape[1]
    shard_rows = gather_plane(*by_half(modin, partner_modin)).reshape(blk_count * block_rows, width)
    qkv_part = jnp.dot(shard_rows, w_qkv, preferred_element_type=jnp.float32).astype(jnp.bfloat16)
    mlp_part = jax.nn.gelu(
        jnp.dot(shard_rows, w_mlp_in, preferred_element_type=jnp.float32), approximate=True
    ).astype(jnp.bfloat16)
    joined = jnp.concatenate([qkv_part, mlp_part], axis=1)
    qkv_cols = joined[:, :qkv_width]
    mlp_act = joined[:, qkv_width:]
    ys, xs = lax.axis_size("y"), lax.axis_size("x")
    by_token = lax.all_to_all(qkv_cols, ("y", "x", "zh"), split_axis=0, concat_axis=1, tiled=True)
    by_token = by_token.reshape(block_rows, ys, xs, 2, -1).swapaxes(2, 3).reshape(block_rows, -1)
    group = ("zl", "zh")
    heads_in = lax.all_to_all(by_token, group, split_axis=1, concat_axis=0, tiled=True)
    query_rows = heads_in.shape[0]
    heads4 = heads_in.reshape(query_rows, local_heads, 3, head_size)
    core_at, y_at, x_at = lax.axis_index("core"), lax.axis_index("y"), lax.axis_index("x")
    digits = (lax.axis_size("zl"), 2, ys, 2, xs, block_rows)
    token_grid = jnp.arange(seq_count * tok_seq, dtype=jnp.int32).reshape(digits)

    def own_queries(grid):
        grid = lax.dynamic_index_in_dim(grid, core_at, axis=1, keepdims=False)
        grid = lax.dynamic_index_in_dim(grid, y_at, axis=1, keepdims=False)
        grid = lax.dynamic_index_in_dim(grid, x_at, axis=2, keepdims=False)
        return grid.reshape((query_rows,) + grid.shape[3:])

    query_ids = own_queries(token_grid)
    query_request = segment_of(query_ids, request_ends)
    angles = angles_of(own_queries(positions.reshape(digits + (-1,))), rope_table(head_size))
    query_rot = rotate(rms_scale(heads4[:, :, 0].astype(jnp.float32), q_gain), angles).astype(
        jnp.bfloat16
    )
    key_rot = rotate(rms_scale(heads4[:, :, 1].astype(jnp.float32), k_gain), angles).astype(
        jnp.bfloat16
    )
    value_rows = heads4[:, :, 2]
    kv_rows = jnp.concatenate([key_rot, value_rows], axis=2)
    key_order = (1, 2, 4, 0, 3, 5)
    key_ids = token_grid.transpose(key_order).reshape(-1)
    key_request = segment_of(key_ids, request_ends)
    kept = key_keep.reshape(digits).transpose(key_order).reshape(-1) == 1
    visible = (query_request[:, None] == key_request[None, :]) & (
        kept[None, :] | (query_ids[:, None] == key_ids[None, :])
    )
    first_core = core_at == 0
    head_out = []
    got = lax.all_to_all(
        jnp.broadcast_to(kv_rows[None], (ys * xs,) + kv_rows.shape), PLANE, 0, 0, tiled=True
    )
    sibling = lax.ppermute(got, "core", SWAP)
    both = jnp.stack([jnp.where(first_core, got, sibling), jnp.where(first_core, sibling, got)])
    both = both.reshape((-1,) + kv_rows.shape[1:])
    for head in range(local_heads):
        key_h = both[:, head, :head_size]
        value_h = both[:, head, head_size:]
        scores = (
            jnp.einsum("qd,kd->qk", query_rot[:, head], key_h, preferred_element_type=jnp.float32)
            * inv_root
        )
        row_high = jnp.max(jnp.where(visible, scores, -1e30), axis=1)
        weights = jnp.where(visible, jnp.exp(scores - row_high[:, None]), 0.0)
        totals = jnp.sum(weights, axis=1)
        mixed = jnp.dot(weights.astype(jnp.bfloat16), value_h, preferred_element_type=jnp.float32)
        head_out.append((mixed / totals[:, None]).astype(jnp.bfloat16))
    attended = jnp.stack(head_out, axis=1)
    attended = attended.reshape(query_rows, local_heads * head_size)
    attn_feats = lax.all_to_all(attended, group, split_axis=0, concat_axis=1, tiled=True)
    attn_feats = attn_feats.reshape(block_rows, ys, 2, xs, -1).swapaxes(2, 3).reshape(block_rows, -1)
    attn_local = lax.all_to_all(attn_feats, ("y", "x", "zh"), split_axis=1, concat_axis=0, tiled=True)
    mlp_out = lax.optimization_barrier(
        jnp.dot(mlp_act, w_mlp_out, preferred_element_type=jnp.float32)
    )
    partial = (jnp.dot(attn_local, w_attn_out, preferred_element_type=jnp.float32) + mlp_out).astype(
        jnp.bfloat16
    )
    summed = reduce_blk(partial)
    return stream + mod_gate * summed


def solution(mesh):
    zl = mesh.shape["seq"] // 2
    ys, xs = 4, mesh.shape["blk"] // 8
    fine = jax.sharding.Mesh(mesh.devices.reshape(zl, 2, ys, 2, xs), SEQ + BLK)
    in_specs = (
        P(SEQ + BLK, None),
        P(),
        P(),
        P(),
        P(),
        P(),
        P(None, BLK),
        P(None, BLK),
        P(),
        P(),
        P(BLK, None),
        P(BLK, None),
    )
    out_specs = P(SEQ + BLK, None)
    return jax.shard_map(body, mesh=fine, in_specs=in_specs, out_specs=out_specs, check_vma=False)
```

```python
import math

import jax
import jax.numpy as jnp
from jax import lax
from jax.sharding import PartitionSpec as P


def rope_table(head_size):
    first_count = head_size // 16
    second = 7 * head_size // 32
    pair_ids = jnp.arange(head_size // 2, dtype=jnp.int32)
    pair_axis = jnp.where(
        pair_ids < first_count, 0, jnp.where(pair_ids < first_count + second, 1, 2)
    )
    pair_local = jnp.where(
        pair_ids < first_count,
        pair_ids,
        jnp.where(
            pair_ids < first_count + second, pair_ids - first_count, pair_ids - first_count - second
        ),
    )
    axis_dims = jnp.where(pair_axis == 0, 2 * first_count, 2 * second)
    frequency = jnp.power(
        jnp.float32(10000.0), -(2 * pair_local).astype(jnp.float32) / axis_dims.astype(jnp.float32)
    )
    return jnp.where(
        jnp.arange(3)[:, None] == pair_axis[None, :], frequency[None, :], jnp.float32(0.0)
    )


def angles_of(places, freq_table):
    return jnp.sum(places.astype(jnp.float32)[:, :, None] * freq_table[None, :, :], axis=1)


def rotate(values, angles):
    paired = values.reshape(values.shape[:-1] + (values.shape[-1] // 2, 2))
    even_part = paired[..., 0]
    odd_part = paired[..., 1]
    cos_part = jnp.cos(angles)[:, None, :]
    sin_part = jnp.sin(angles)[:, None, :]
    turned = jnp.stack(
        [cos_part * even_part - sin_part * odd_part, sin_part * even_part + cos_part * odd_part],
        axis=-1,
    )
    return turned.reshape(values.shape)


def rms_scale(values, gain_vec):
    return values * lax.rsqrt(jnp.mean(values * values, axis=-1, keepdims=True) + 1e-06) * gain_vec


def segment_of(row_ids, request_ends):
    return jnp.sum((row_ids[:, None] >= request_ends[None, :]).astype(jnp.int32), axis=1)


def spread_rows(row_ids, query_rows, block_rows, tok_seq):
    owner = row_ids // query_rows
    within = row_ids % query_rows
    return within // block_rows * tok_seq + owner * block_rows + within % block_rows


SEQ = ("zl", "core")
BLK = ("y", "zh", "x")
PLANE = ("y", "x")
SWAP = [(0, 1), (1, 0)]


def by_half(mine, other):
    first = lax.axis_index("zh") == 0
    return jnp.where(first, mine, other), jnp.where(first, other, mine)


def gather_plane(low, high):
    pair = jnp.stack([low, high])
    plane = lax.axis_size("y") * lax.axis_size("x")
    got = lax.all_to_all(jnp.broadcast_to(pair[None], (plane,) + pair.shape), PLANE, 0, 0, tiled=True)
    return got.reshape((lax.axis_size("y"), lax.axis_size("x"), 2) + low.shape)


def reduce_blk(y):
    plane = lax.axis_size("y") * lax.axis_size("x")
    done = []
    for cols in jnp.split(y, 2, axis=1):
        pieces = cols.reshape((plane, 2, y.shape[0] // (plane * 2)) + cols.shape[1:])
        got = lax.all_to_all(pieces, PLANE, 0, 0, tiled=True)
        part = jnp.sum(got.astype(jnp.float32), axis=0)
        mine, theirs = by_half(part[0], part[1])
        done.append(mine + lax.ppermute(theirs, "zh", SWAP))
    return jnp.concatenate(done, axis=1)


def body(
    stream,
    key_keep,
    positions,
    lengths,
    step_index,
    mod_table,
    w_qkv,
    w_mlp_in,
    q_gain,
    k_gain,
    w_attn_out,
    w_mlp_out,
):
    blk_count = lax.axis_size(BLK)
    seq_count = lax.axis_size(SEQ)
    seq_at = lax.axis_index(SEQ)
    blk_at = lax.axis_index(BLK)
    block_rows = stream.shape[0]
    width = stream.shape[1]
    tok_seq = block_rows * blk_count
    head_size = q_gain.shape[0]
    local_heads = width // head_size // seq_count
    requests = mod_table.shape[0]
    step_total = mod_table.shape[1]
    inv_root = 1.0 / math.sqrt(head_size)
    request_ends = jnp.cumsum(lengths)
    partner_blk = blk_at + lax.axis_size("x") * (1 - 2 * lax.axis_index("zh"))
    partner_stream = lax.ppermute(stream, "zh", SWAP)
    step_pick = (jnp.arange(step_total, dtype=jnp.int32)[None, :] == step_index[:, None]).astype(
        jnp.bfloat16
    )
    modulation = jnp.einsum(
        "rs,rsk->rk",
        step_pick,
        mod_table.reshape(requests, step_total, 3 * width),
        preferred_element_type=jnp.float32,
    )

    def modulated(rows, row_blk):
        row_ids = seq_at * tok_seq + row_blk * block_rows + jnp.arange(block_rows, dtype=jnp.int32)
        row_request = segment_of(row_ids, request_ends)
        member = (row_request[:, None] == jnp.arange(requests, dtype=jnp.int32)[None, :]).astype(
            jnp.float32
        )
        token_mod = jnp.dot(member, modulation, precision=lax.Precision.HIGHEST)
        mod_shift = token_mod[:, :width]
        mod_scale = token_mod[:, width : 2 * width]
        row_mean = jnp.mean(rows, axis=1, keepdims=True)
        centered = rows - row_mean
        row_var = jnp.mean(centered * centered, axis=1, keepdims=True)
        normed = centered * lax.rsqrt(row_var + 1e-06)
        return ((1.0 + mod_scale) * normed + mod_shift).astype(jnp.bfloat16), token_mod[:, 2 * width :]

    modin, mod_gate = modulated(stream, blk_at)
    partner_modin, _ = modulated(partner_stream, partner_blk)
    qkv_width = w_qkv.shape[1]
    shard_rows = gather_plane(*by_half(modin, partner_modin)).reshape(blk_count * block_rows, width)
    qkv_part = jnp.dot(shard_rows, w_qkv, preferred_element_type=jnp.float32).astype(jnp.bfloat16)
    mlp_part = jax.nn.gelu(
        jnp.dot(shard_rows, w_mlp_in, preferred_element_type=jnp.float32), approximate=True
    ).astype(jnp.bfloat16)
    joined = jnp.concatenate([qkv_part, mlp_part], axis=1)
    qkv_cols = joined[:, :qkv_width]
    mlp_act = joined[:, qkv_width:]
    ys, xs = lax.axis_size("y"), lax.axis_size("x")
    by_token = lax.all_to_all(qkv_cols, ("y", "x", "zh"), split_axis=0, concat_axis=1, tiled=True)
    by_token = by_token.reshape(block_rows, ys, xs, 2, -1).swapaxes(2, 3).reshape(block_rows, -1)
    group = ("zl", "zh")
    heads_in = lax.all_to_all(by_token, group, split_axis=1, concat_axis=0, tiled=True)
    query_rows = heads_in.shape[0]
    heads4 = heads_in.reshape(query_rows, local_heads, 3, head_size)
    core_at, y_at, x_at = lax.axis_index("core"), lax.axis_index("y"), lax.axis_index("x")
    digits = (lax.axis_size("zl"), 2, ys, 2, xs, block_rows)
    token_grid = jnp.arange(seq_count * tok_seq, dtype=jnp.int32).reshape(digits)

    def own_queries(grid):
        grid = lax.dynamic_index_in_dim(grid, core_at, axis=1, keepdims=False)
        grid = lax.dynamic_index_in_dim(grid, y_at, axis=1, keepdims=False)
        grid = lax.dynamic_index_in_dim(grid, x_at, axis=2, keepdims=False)
        return grid.reshape((query_rows,) + grid.shape[3:])

    query_ids = own_queries(token_grid)
    query_request = segment_of(query_ids, request_ends)
    angles = angles_of(own_queries(positions.reshape(digits + (-1,))), rope_table(head_size))
    query_rot = rotate(rms_scale(heads4[:, :, 0].astype(jnp.float32), q_gain), angles).astype(
        jnp.bfloat16
    )
    key_rot = rotate(rms_scale(heads4[:, :, 1].astype(jnp.float32), k_gain), angles).astype(
        jnp.bfloat16
    )
    value_rows = heads4[:, :, 2]
    kv_rows = jnp.concatenate([key_rot, value_rows], axis=2)
    key_order = (1, 2, 4, 0, 3, 5)
    key_ids = token_grid.transpose(key_order).reshape(-1)
    key_request = segment_of(key_ids, request_ends)
    kept = key_keep.reshape(digits).transpose(key_order).reshape(-1) == 1
    visible = (query_request[:, None] == key_request[None, :]) & (
        kept[None, :] | (query_ids[:, None] == key_ids[None, :])
    )
    first_core = core_at == 0
    head_out = []
    got = lax.all_to_all(
        jnp.broadcast_to(kv_rows[None], (ys * xs,) + kv_rows.shape), PLANE, 0, 0, tiled=True
    )
    sibling = lax.ppermute(got, "core", SWAP)
    both = jnp.stack([jnp.where(first_core, got, sibling), jnp.where(first_core, sibling, got)])
    both = both.reshape((-1,) + kv_rows.shape[1:])
    for head in range(local_heads):
        key_h = both[:, head, :head_size]
        value_h = both[:, head, head_size:]
        scores = (
            jnp.einsum("qd,kd->qk", query_rot[:, head], key_h, preferred_element_type=jnp.float32)
            * inv_root
        )
        row_high = jnp.max(jnp.where(visible, scores, -1e30), axis=1)
        weights = jnp.where(visible, jnp.exp(scores - row_high[:, None]), 0.0)
        totals = jnp.sum(weights, axis=1)
        mixed = jnp.dot(weights.astype(jnp.bfloat16), value_h, preferred_element_type=jnp.float32)
        head_out.append((mixed / totals[:, None]).astype(jnp.bfloat16))
    attended = jnp.stack(head_out, axis=1)
    attended = attended.reshape(query_rows, local_heads * head_size)
    attn_feats = lax.all_to_all(attended, group, split_axis=0, concat_axis=1, tiled=True)
    attn_feats = attn_feats.reshape(block_rows, ys, 2, xs, -1).swapaxes(2, 3).reshape(block_rows, -1)
    attn_local = lax.all_to_all(attn_feats, ("y", "x", "zh"), split_axis=1, concat_axis=0, tiled=True)
    mlp_out = lax.optimization_barrier(
        jnp.dot(mlp_act, w_mlp_out, preferred_element_type=jnp.float32)
    )
    partial = (jnp.dot(attn_local, w_attn_out, preferred_element_type=jnp.float32) + mlp_out).astype(
        jnp.bfloat16
    )
    summed = reduce_blk(partial)
    return stream + mod_gate * summed


def solution(mesh):
    zl = mesh.shape["seq"] // 2
    ys, xs = 4, mesh.shape["blk"] // 8
    fine = jax.sharding.Mesh(mesh.devices.reshape(zl, 2, ys, 2, xs), SEQ + BLK)
    in_specs = (
        P(SEQ + BLK, None),
        P(),
        P(),
        P(),
        P(),
        P(),
        P(None, BLK),
        P(None, BLK),
        P(),
        P(),
        P(BLK, None),
        P(BLK, None),
    )
    out_specs = P(SEQ + BLK, None)
    return jax.shard_map(body, mesh=fine, in_specs=in_specs, out_specs=out_specs, check_vma=False)
```

```python
import math

import jax
import jax.numpy as jnp
from jax import lax
from jax.sharding import PartitionSpec as P


def rope_table(head_size):
    first_count = head_size // 16
    second = 7 * head_size // 32
    pair_ids = jnp.arange(head_size // 2, dtype=jnp.int32)
    pair_axis = jnp.where(
        pair_ids < first_count, 0, jnp.where(pair_ids < first_count + second, 1, 2)
    )
    pair_local = jnp.where(
        pair_ids < first_count,
        pair_ids,
        jnp.where(
            pair_ids < first_count + second, pair_ids - first_count, pair_ids - first_count - second
        ),
    )
    axis_dims = jnp.where(pair_axis == 0, 2 * first_count, 2 * second)
    frequency = jnp.power(
        jnp.float32(10000.0), -(2 * pair_local).astype(jnp.float32) / axis_dims.astype(jnp.float32)
    )
    return jnp.where(
        jnp.arange(3)[:, None] == pair_axis[None, :], frequency[None, :], jnp.float32(0.0)
    )


def angles_of(places, freq_table):
    return jnp.sum(places.astype(jnp.float32)[:, :, None] * freq_table[None, :, :], axis=1)


def rotate(values, angles):
    paired = values.reshape(values.shape[:-1] + (values.shape[-1] // 2, 2))
    even_part = paired[..., 0]
    odd_part = paired[..., 1]
    cos_part = jnp.cos(angles)[:, None, :]
    sin_part = jnp.sin(angles)[:, None, :]
    turned = jnp.stack(
        [cos_part * even_part - sin_part * odd_part, sin_part * even_part + cos_part * odd_part],
        axis=-1,
    )
    return turned.reshape(values.shape)


def rms_scale(values, gain_vec):
    return values * lax.rsqrt(jnp.mean(values * values, axis=-1, keepdims=True) + 1e-06) * gain_vec


def segment_of(row_ids, request_ends):
    return jnp.sum((row_ids[:, None] >= request_ends[None, :]).astype(jnp.int32), axis=1)


def spread_rows(row_ids, query_rows, block_rows, tok_seq):
    owner = row_ids // query_rows
    within = row_ids % query_rows
    return within // block_rows * tok_seq + owner * block_rows + within % block_rows


SEQ = ("zl", "core")
BLK = ("y", "zh", "x")
PLANE = ("y", "x")
SWAP = [(0, 1), (1, 0)]


def by_half(mine, other):
    first = lax.axis_index("zh") == 0
    return jnp.where(first, mine, other), jnp.where(first, other, mine)


def gather_plane(low, high):
    pair = jnp.stack([low, high])
    plane = lax.axis_size("y") * lax.axis_size("x")
    got = lax.all_to_all(jnp.broadcast_to(pair[None], (plane,) + pair.shape), PLANE, 0, 0, tiled=True)
    return got.reshape((lax.axis_size("y"), lax.axis_size("x"), 2) + low.shape)


def reduce_blk(y):
    plane = lax.axis_size("y") * lax.axis_size("x")
    pieces = y.reshape((plane, 2, y.shape[0] // (plane * 2)) + y.shape[1:])
    got = lax.all_to_all(pieces, PLANE, 0, 0, tiled=True)
    part = jnp.sum(got.astype(jnp.float32), axis=0)
    mine, theirs = by_half(part[0], part[1])
    return mine + lax.ppermute(theirs.astype(jnp.bfloat16), "zh", SWAP).astype(jnp.float32)


def body(
    stream,
    key_keep,
    positions,
    lengths,
    step_index,
    mod_table,
    w_qkv,
    w_mlp_in,
    q_gain,
    k_gain,
    w_attn_out,
    w_mlp_out,
):
    blk_count = lax.axis_size(BLK)
    seq_count = lax.axis_size(SEQ)
    seq_at = lax.axis_index(SEQ)
    blk_at = lax.axis_index(BLK)
    block_rows = stream.shape[0]
    width = stream.shape[1]
    tok_seq = block_rows * blk_count
    head_size = q_gain.shape[0]
    local_heads = width // head_size // seq_count
    requests = mod_table.shape[0]
    step_total = mod_table.shape[1]
    inv_root = 1.0 / math.sqrt(head_size)
    request_ends = jnp.cumsum(lengths)
    partner_blk = blk_at + lax.axis_size("x") * (1 - 2 * lax.axis_index("zh"))
    partner_stream = lax.ppermute(stream, "zh", SWAP)
    step_pick = (jnp.arange(step_total, dtype=jnp.int32)[None, :] == step_index[:, None]).astype(
        jnp.bfloat16
    )
    modulation = jnp.einsum(
        "rs,rsk->rk",
        step_pick,
        mod_table.reshape(requests, step_total, 3 * width),
        preferred_element_type=jnp.float32,
    )

    def modulated(rows, row_blk):
        row_ids = seq_at * tok_seq + row_blk * block_rows + jnp.arange(block_rows, dtype=jnp.int32)
        row_request = segment_of(row_ids, request_ends)
        member = (row_request[:, None] == jnp.arange(requests, dtype=jnp.int32)[None, :]).astype(
            jnp.float32
        )
        token_mod = jnp.dot(member, modulation, precision=lax.Precision.HIGHEST)
        mod_shift = token_mod[:, :width]
        mod_scale = token_mod[:, width : 2 * width]
        row_mean = jnp.mean(rows, axis=1, keepdims=True)
        centered = rows - row_mean
        row_var = jnp.mean(centered * centered, axis=1, keepdims=True)
        normed = centered * lax.rsqrt(row_var + 1e-06)
        return ((1.0 + mod_scale) * normed + mod_shift).astype(jnp.bfloat16), token_mod[:, 2 * width :]

    modin, mod_gate = modulated(stream, blk_at)
    partner_modin, _ = modulated(partner_stream, partner_blk)
    qkv_width = w_qkv.shape[1]
    shard_rows = gather_plane(*by_half(modin, partner_modin)).reshape(blk_count * block_rows, width)
    qkv_part = jnp.dot(shard_rows, w_qkv, preferred_element_type=jnp.float32).astype(jnp.bfloat16)
    mlp_part = jax.nn.gelu(
        jnp.dot(shard_rows, w_mlp_in, preferred_element_type=jnp.float32), approximate=True
    ).astype(jnp.bfloat16)
    joined = jnp.concatenate([qkv_part, mlp_part], axis=1)
    qkv_cols = joined[:, :qkv_width]
    mlp_act = joined[:, qkv_width:]
    ys, xs = lax.axis_size("y"), lax.axis_size("x")
    by_token = lax.all_to_all(qkv_cols, ("y", "x", "zh"), split_axis=0, concat_axis=1, tiled=True)
    by_token = by_token.reshape(block_rows, ys, xs, 2, -1).swapaxes(2, 3).reshape(block_rows, -1)
    group = ("zl", "zh")
    heads_in = lax.all_to_all(by_token, group, split_axis=1, concat_axis=0, tiled=True)
    query_rows = heads_in.shape[0]
    heads4 = heads_in.reshape(query_rows, local_heads, 3, head_size)
    core_at, y_at, x_at = lax.axis_index("core"), lax.axis_index("y"), lax.axis_index("x")
    digits = (lax.axis_size("zl"), 2, ys, 2, xs, block_rows)
    token_grid = jnp.arange(seq_count * tok_seq, dtype=jnp.int32).reshape(digits)

    def own_queries(grid):
        grid = lax.dynamic_index_in_dim(grid, core_at, axis=1, keepdims=False)
        grid = lax.dynamic_index_in_dim(grid, y_at, axis=1, keepdims=False)
        grid = lax.dynamic_index_in_dim(grid, x_at, axis=2, keepdims=False)
        return grid.reshape((query_rows,) + grid.shape[3:])

    query_ids = own_queries(token_grid)
    query_request = segment_of(query_ids, request_ends)
    angles = angles_of(own_queries(positions.reshape(digits + (-1,))), rope_table(head_size))
    query_rot = rotate(rms_scale(heads4[:, :, 0].astype(jnp.float32), q_gain), angles).astype(
        jnp.bfloat16
    )
    key_rot = rotate(rms_scale(heads4[:, :, 1].astype(jnp.float32), k_gain), angles).astype(
        jnp.bfloat16
    )
    value_rows = heads4[:, :, 2]
    kv_rows = jnp.concatenate([key_rot, value_rows], axis=2)
    key_order = (1, 2, 4, 0, 3, 5)
    key_ids = token_grid.transpose(key_order).reshape(-1)
    key_request = segment_of(key_ids, request_ends)
    kept = key_keep.reshape(digits).transpose(key_order).reshape(-1) == 1
    visible = (query_request[:, None] == key_request[None, :]) & (
        kept[None, :] | (query_ids[:, None] == key_ids[None, :])
    )
    first_core = core_at == 0
    head_out = []
    got = lax.all_to_all(
        jnp.broadcast_to(kv_rows[None], (ys * xs,) + kv_rows.shape), PLANE, 0, 0, tiled=True
    )
    sibling = lax.ppermute(got, "core", SWAP)
    both = jnp.stack([jnp.where(first_core, got, sibling), jnp.where(first_core, sibling, got)])
    both = both.reshape((-1,) + kv_rows.shape[1:])
    for head in range(local_heads):
        key_h = both[:, head, :head_size]
        value_h = both[:, head, head_size:]
        scores = (
            jnp.einsum("qd,kd->qk", query_rot[:, head], key_h, preferred_element_type=jnp.float32)
            * inv_root
        )
        row_high = jnp.max(jnp.where(visible, scores, -1e30), axis=1)
        weights = jnp.where(visible, jnp.exp(scores - row_high[:, None]), 0.0)
        totals = jnp.sum(weights, axis=1)
        mixed = jnp.dot(weights.astype(jnp.bfloat16), value_h, preferred_element_type=jnp.float32)
        head_out.append((mixed / totals[:, None]).astype(jnp.bfloat16))
    attended = jnp.stack(head_out, axis=1)
    attended = attended.reshape(query_rows, local_heads * head_size)
    attn_feats = lax.all_to_all(attended, group, split_axis=0, concat_axis=1, tiled=True)
    attn_feats = attn_feats.reshape(block_rows, ys, 2, xs, -1).swapaxes(2, 3).reshape(block_rows, -1)
    attn_local = lax.all_to_all(attn_feats, ("y", "x", "zh"), split_axis=1, concat_axis=0, tiled=True)
    mlp_out = lax.optimization_barrier(
        jnp.dot(mlp_act, w_mlp_out, preferred_element_type=jnp.float32)
    )
    partial = (jnp.dot(attn_local, w_attn_out, preferred_element_type=jnp.float32) + mlp_out).astype(
        jnp.bfloat16
    )
    summed = reduce_blk(partial)
    return stream + mod_gate * summed


def solution(mesh):
    zl = mesh.shape["seq"] // 2
    ys, xs = 4, mesh.shape["blk"] // 8
    fine = jax.sharding.Mesh(mesh.devices.reshape(zl, 2, ys, 2, xs), SEQ + BLK)
    in_specs = (
        P(SEQ + BLK, None),
        P(),
        P(),
        P(),
        P(),
        P(),
        P(None, BLK),
        P(None, BLK),
        P(),
        P(),
        P(BLK, None),
        P(BLK, None),
    )
    out_specs = P(SEQ + BLK, None)
    return jax.shard_map(body, mesh=fine, in_specs=in_specs, out_specs=out_specs, check_vma=False)
```

```python
import math

import jax
import jax.numpy as jnp
from jax import lax
from jax.sharding import PartitionSpec as P


def rope_table(head_size):
    first_count = head_size // 16
    second = 7 * head_size // 32
    pair_ids = jnp.arange(head_size // 2, dtype=jnp.int32)
    pair_axis = jnp.where(
        pair_ids < first_count, 0, jnp.where(pair_ids < first_count + second, 1, 2)
    )
    pair_local = jnp.where(
        pair_ids < first_count,
        pair_ids,
        jnp.where(
            pair_ids < first_count + second, pair_ids - first_count, pair_ids - first_count - second
        ),
    )
    axis_dims = jnp.where(pair_axis == 0, 2 * first_count, 2 * second)
    frequency = jnp.power(
        jnp.float32(10000.0), -(2 * pair_local).astype(jnp.float32) / axis_dims.astype(jnp.float32)
    )
    return jnp.where(
        jnp.arange(3)[:, None] == pair_axis[None, :], frequency[None, :], jnp.float32(0.0)
    )


def angles_of(places, freq_table):
    return jnp.sum(places.astype(jnp.float32)[:, :, None] * freq_table[None, :, :], axis=1)


def rotate(values, angles):
    paired = values.reshape(values.shape[:-1] + (values.shape[-1] // 2, 2))
    even_part = paired[..., 0]
    odd_part = paired[..., 1]
    cos_part = jnp.cos(angles)[:, None, :]
    sin_part = jnp.sin(angles)[:, None, :]
    turned = jnp.stack(
        [cos_part * even_part - sin_part * odd_part, sin_part * even_part + cos_part * odd_part],
        axis=-1,
    )
    return turned.reshape(values.shape)


def rms_scale(values, gain_vec):
    return values * lax.rsqrt(jnp.mean(values * values, axis=-1, keepdims=True) + 1e-06) * gain_vec


def segment_of(row_ids, request_ends):
    return jnp.sum((row_ids[:, None] >= request_ends[None, :]).astype(jnp.int32), axis=1)


def spread_rows(row_ids, query_rows, block_rows, tok_seq):
    owner = row_ids // query_rows
    within = row_ids % query_rows
    return within // block_rows * tok_seq + owner * block_rows + within % block_rows


SEQ = ("zl", "core")
BLK = ("y", "zh", "x")
PLANE = ("y", "x")
SWAP = [(0, 1), (1, 0)]


def by_half(mine, other):
    first = lax.axis_index("zh") == 0
    return jnp.where(first, mine, other), jnp.where(first, other, mine)


def gather_plane(low, high):
    pair = jnp.stack([low, high])
    plane = lax.axis_size("y") * lax.axis_size("x")
    got = lax.all_to_all(jnp.broadcast_to(pair[None], (plane,) + pair.shape), PLANE, 0, 0, tiled=True)
    return got.reshape((lax.axis_size("y"), lax.axis_size("x"), 2) + low.shape)


def reduce_blk(y):
    plane = lax.axis_size("y") * lax.axis_size("x")
    pieces = y.reshape((plane, 2, y.shape[0] // (plane * 2)) + y.shape[1:])
    got = lax.all_to_all(pieces, PLANE, 0, 0, tiled=True)
    part = jnp.sum(got.astype(jnp.float32), axis=0)
    mine, theirs = by_half(part[0], part[1])
    return mine + lax.ppermute(theirs.astype(jnp.bfloat16), "zh", SWAP).astype(jnp.float32)


def body(
    stream,
    key_keep,
    positions,
    lengths,
    step_index,
    mod_table,
    w_qkv,
    w_mlp_in,
    q_gain,
    k_gain,
    w_attn_out,
    w_mlp_out,
):
    blk_count = lax.axis_size(BLK)
    seq_count = lax.axis_size(SEQ)
    seq_at = lax.axis_index(SEQ)
    blk_at = lax.axis_index(BLK)
    block_rows = stream.shape[0]
    width = stream.shape[1]
    tok_seq = block_rows * blk_count
    head_size = q_gain.shape[0]
    local_heads = width // head_size // seq_count
    requests = mod_table.shape[0]
    step_total = mod_table.shape[1]
    inv_root = 1.0 / math.sqrt(head_size)
    request_ends = jnp.cumsum(lengths)
    partner_blk = blk_at + lax.axis_size("x") * (1 - 2 * lax.axis_index("zh"))
    partner_stream = lax.ppermute(stream, "zh", SWAP)
    step_pick = (jnp.arange(step_total, dtype=jnp.int32)[None, :] == step_index[:, None]).astype(
        jnp.bfloat16
    )
    modulation = jnp.einsum(
        "rs,rsk->rk",
        step_pick,
        mod_table.reshape(requests, step_total, 3 * width),
        preferred_element_type=jnp.float32,
    )

    def modulated(rows, row_blk):
        row_ids = seq_at * tok_seq + row_blk * block_rows + jnp.arange(block_rows, dtype=jnp.int32)
        row_request = segment_of(row_ids, request_ends)
        member = (row_request[:, None] == jnp.arange(requests, dtype=jnp.int32)[None, :]).astype(
            jnp.float32
        )
        token_mod = jnp.dot(member, modulation, precision=lax.Precision.HIGHEST)
        mod_shift = token_mod[:, :width]
        mod_scale = token_mod[:, width : 2 * width]
        row_mean = jnp.mean(rows, axis=1, keepdims=True)
        centered = rows - row_mean
        row_var = jnp.mean(centered * centered, axis=1, keepdims=True)
        normed = centered * lax.rsqrt(row_var + 1e-06)
        return ((1.0 + mod_scale) * normed + mod_shift).astype(jnp.bfloat16), token_mod[:, 2 * width :]

    modin, mod_gate = modulated(stream, blk_at)
    partner_modin, _ = modulated(partner_stream, partner_blk)
    qkv_width = w_qkv.shape[1]
    shard_rows = gather_plane(*by_half(modin, partner_modin)).reshape(blk_count * block_rows, width)
    qkv_part = jnp.dot(shard_rows, w_qkv, preferred_element_type=jnp.float32).astype(jnp.bfloat16)
    mlp_part = jax.nn.gelu(
        jnp.dot(shard_rows, w_mlp_in, preferred_element_type=jnp.float32), approximate=True
    ).astype(jnp.bfloat16)
    joined = jnp.concatenate([qkv_part, mlp_part], axis=1)
    qkv_cols = joined[:, :qkv_width]
    mlp_act = joined[:, qkv_width:]
    ys, xs = lax.axis_size("y"), lax.axis_size("x")
    by_token = lax.all_to_all(qkv_cols, ("y", "x", "zh"), split_axis=0, concat_axis=1, tiled=True)
    by_token = by_token.reshape(block_rows, ys, xs, 2, -1).swapaxes(2, 3).reshape(block_rows, -1)
    group = ("zl", "zh")
    heads_in = lax.all_to_all(by_token, group, split_axis=1, concat_axis=0, tiled=True)
    query_rows = heads_in.shape[0]
    heads4 = heads_in.reshape(query_rows, local_heads, 3, head_size)
    core_at, y_at, x_at = lax.axis_index("core"), lax.axis_index("y"), lax.axis_index("x")
    digits = (lax.axis_size("zl"), 2, ys, 2, xs, block_rows)
    token_grid = jnp.arange(seq_count * tok_seq, dtype=jnp.int32).reshape(digits)

    def own_queries(grid):
        grid = lax.dynamic_index_in_dim(grid, core_at, axis=1, keepdims=False)
        grid = lax.dynamic_index_in_dim(grid, y_at, axis=1, keepdims=False)
        grid = lax.dynamic_index_in_dim(grid, x_at, axis=2, keepdims=False)
        return grid.reshape((query_rows,) + grid.shape[3:])

    query_ids = own_queries(token_grid)
    query_request = segment_of(query_ids, request_ends)
    angles = angles_of(own_queries(positions.reshape(digits + (-1,))), rope_table(head_size))
    query_rot = rotate(rms_scale(heads4[:, :, 0].astype(jnp.float32), q_gain), angles).astype(
        jnp.bfloat16
    )
    key_rot = rotate(rms_scale(heads4[:, :, 1].astype(jnp.float32), k_gain), angles).astype(
        jnp.bfloat16
    )
    value_rows = heads4[:, :, 2]
    kv_rows = jnp.concatenate([key_rot, value_rows], axis=2)
    key_order = (1, 2, 4, 0, 3, 5)
    first_core = core_at == 0
    key_grid = token_grid.transpose(key_order)
    key_ids = jnp.where(first_core, key_grid, key_grid[::-1]).reshape(-1)
    key_request = segment_of(key_ids, request_ends)
    keep_grid = key_keep.reshape(digits).transpose(key_order)
    kept = jnp.where(first_core, keep_grid, keep_grid[::-1]).reshape(-1) == 1
    visible = (query_request[:, None] == key_request[None, :]) & (
        kept[None, :] | (query_ids[:, None] == key_ids[None, :])
    )
    head_out = []
    got = lax.all_to_all(
        jnp.broadcast_to(kv_rows[None], (ys * xs,) + kv_rows.shape), PLANE, 0, 0, tiled=True
    )
    sibling = lax.ppermute(got, "core", SWAP)
    both = jnp.stack([got, sibling])
    both = both.reshape((-1,) + kv_rows.shape[1:])
    for head in range(local_heads):
        key_h = both[:, head, :head_size]
        value_h = both[:, head, head_size:]
        scores = (
            jnp.einsum("qd,kd->qk", query_rot[:, head], key_h, preferred_element_type=jnp.float32)
            * inv_root
        )
        row_high = jnp.max(jnp.where(visible, scores, -1e30), axis=1)
        weights = jnp.where(visible, jnp.exp(scores - row_high[:, None]), 0.0)
        totals = jnp.sum(weights, axis=1)
        mixed = jnp.dot(weights.astype(jnp.bfloat16), value_h, preferred_element_type=jnp.float32)
        head_out.append((mixed / totals[:, None]).astype(jnp.bfloat16))
    attended = jnp.stack(head_out, axis=1)
    attended = attended.reshape(query_rows, local_heads * head_size)
    attn_feats = lax.all_to_all(attended, group, split_axis=0, concat_axis=1, tiled=True)
    attn_feats = attn_feats.reshape(block_rows, ys, 2, xs, -1).swapaxes(2, 3).reshape(block_rows, -1)
    attn_local = lax.all_to_all(attn_feats, ("y", "x", "zh"), split_axis=1, concat_axis=0, tiled=True)
    mlp_out = lax.optimization_barrier(
        jnp.dot(mlp_act, w_mlp_out, preferred_element_type=jnp.float32)
    )
    partial = (jnp.dot(attn_local, w_attn_out, preferred_element_type=jnp.float32) + mlp_out).astype(
        jnp.bfloat16
    )
    summed = reduce_blk(partial)
    return stream + mod_gate * summed


def solution(mesh):
    zl = mesh.shape["seq"] // 2
    ys, xs = 4, mesh.shape["blk"] // 8
    fine = jax.sharding.Mesh(mesh.devices.reshape(zl, 2, ys, 2, xs), SEQ + BLK)
    in_specs = (
        P(SEQ + BLK, None),
        P(),
        P(),
        P(),
        P(),
        P(),
        P(None, BLK),
        P(None, BLK),
        P(),
        P(),
        P(BLK, None),
        P(BLK, None),
    )
    out_specs = P(SEQ + BLK, None)
    return jax.shard_map(body, mesh=fine, in_specs=in_specs, out_specs=out_specs, check_vma=False)
```

```python
import math

import jax
import jax.numpy as jnp
from jax import lax
from jax.sharding import PartitionSpec as P


def rope_table(head_size):
    first_count = head_size // 16
    second = 7 * head_size // 32
    pair_ids = jnp.arange(head_size // 2, dtype=jnp.int32)
    pair_axis = jnp.where(
        pair_ids < first_count, 0, jnp.where(pair_ids < first_count + second, 1, 2)
    )
    pair_local = jnp.where(
        pair_ids < first_count,
        pair_ids,
        jnp.where(
            pair_ids < first_count + second, pair_ids - first_count, pair_ids - first_count - second
        ),
    )
    axis_dims = jnp.where(pair_axis == 0, 2 * first_count, 2 * second)
    frequency = jnp.power(
        jnp.float32(10000.0), -(2 * pair_local).astype(jnp.float32) / axis_dims.astype(jnp.float32)
    )
    return jnp.where(
        jnp.arange(3)[:, None] == pair_axis[None, :], frequency[None, :], jnp.float32(0.0)
    )


def angles_of(places, freq_table):
    return jnp.sum(places.astype(jnp.float32)[:, :, None] * freq_table[None, :, :], axis=1)


def rotate(values, angles):
    paired = values.reshape(values.shape[:-1] + (values.shape[-1] // 2, 2))
    even_part = paired[..., 0]
    odd_part = paired[..., 1]
    cos_part = jnp.cos(angles)[:, None, :]
    sin_part = jnp.sin(angles)[:, None, :]
    turned = jnp.stack(
        [cos_part * even_part - sin_part * odd_part, sin_part * even_part + cos_part * odd_part],
        axis=-1,
    )
    return turned.reshape(values.shape)


def rms_scale(values, gain_vec):
    return values * lax.rsqrt(jnp.mean(values * values, axis=-1, keepdims=True) + 1e-06) * gain_vec


def segment_of(row_ids, request_ends):
    return jnp.sum((row_ids[:, None] >= request_ends[None, :]).astype(jnp.int32), axis=1)


def spread_rows(row_ids, query_rows, block_rows, tok_seq):
    owner = row_ids // query_rows
    within = row_ids % query_rows
    return within // block_rows * tok_seq + owner * block_rows + within % block_rows


SEQ = ("zl", "core")
BLK = ("y", "zh", "x")
PLANE = ("y", "x")
SWAP = [(0, 1), (1, 0)]


def by_half(mine, other):
    first = lax.axis_index("zh") == 0
    return jnp.where(first, mine, other), jnp.where(first, other, mine)


def gather_plane(low, high):
    pair = jnp.stack([low, high])
    plane = lax.axis_size("y") * lax.axis_size("x")
    got = lax.all_to_all(jnp.broadcast_to(pair[None], (plane,) + pair.shape), PLANE, 0, 0, tiled=True)
    return got.reshape((lax.axis_size("y"), lax.axis_size("x"), 2) + low.shape)


def reduce_blk(y):
    plane = lax.axis_size("y") * lax.axis_size("x")
    pieces = y.reshape((plane, 2, y.shape[0] // (plane * 2)) + y.shape[1:])
    got = lax.all_to_all(pieces, PLANE, 0, 0, tiled=True)
    part = jnp.sum(got.astype(jnp.float32), axis=0)
    mine, theirs = by_half(part[0], part[1])
    return mine + lax.ppermute(theirs.astype(jnp.bfloat16), "zh", SWAP).astype(jnp.float32)


def body(
    stream,
    key_keep,
    positions,
    lengths,
    step_index,
    mod_table,
    w_qkv,
    w_mlp_in,
    q_gain,
    k_gain,
    w_attn_out,
    w_mlp_out,
):
    blk_count = lax.axis_size(BLK)
    seq_count = lax.axis_size(SEQ)
    seq_at = lax.axis_index(SEQ)
    blk_at = lax.axis_index(BLK)
    block_rows = stream.shape[0]
    width = stream.shape[1]
    tok_seq = block_rows * blk_count
    head_size = q_gain.shape[0]
    local_heads = width // head_size // seq_count
    requests = mod_table.shape[0]
    step_total = mod_table.shape[1]
    inv_root = 1.0 / math.sqrt(head_size)
    request_ends = jnp.cumsum(lengths)
    partner_blk = blk_at + lax.axis_size("x") * (1 - 2 * lax.axis_index("zh"))
    partner_stream = lax.ppermute(stream, "zh", SWAP)
    step_pick = (jnp.arange(step_total, dtype=jnp.int32)[None, :] == step_index[:, None]).astype(
        jnp.bfloat16
    )
    modulation = jnp.einsum(
        "rs,rsk->rk",
        step_pick,
        mod_table.reshape(requests, step_total, 3 * width),
        preferred_element_type=jnp.float32,
    )

    def modulated(rows, row_blk):
        row_ids = seq_at * tok_seq + row_blk * block_rows + jnp.arange(block_rows, dtype=jnp.int32)
        row_request = segment_of(row_ids, request_ends)
        member = (row_request[:, None] == jnp.arange(requests, dtype=jnp.int32)[None, :]).astype(
            jnp.float32
        )
        token_mod = jnp.dot(member, modulation, precision=lax.Precision.HIGHEST)
        mod_shift = token_mod[:, :width]
        mod_scale = token_mod[:, width : 2 * width]
        row_mean = jnp.mean(rows, axis=1, keepdims=True)
        centered = rows - row_mean
        row_var = jnp.mean(centered * centered, axis=1, keepdims=True)
        normed = centered * lax.rsqrt(row_var + 1e-06)
        return ((1.0 + mod_scale) * normed + mod_shift).astype(jnp.bfloat16), token_mod[:, 2 * width :]

    modin, mod_gate = modulated(stream, blk_at)
    partner_modin, _ = modulated(partner_stream, partner_blk)
    qkv_width = w_qkv.shape[1]
    shard_rows = gather_plane(*by_half(modin, partner_modin)).reshape(blk_count * block_rows, width)
    qkv_part = jnp.dot(shard_rows, w_qkv, preferred_element_type=jnp.float32).astype(jnp.bfloat16)
    mlp_part = jax.nn.gelu(
        jnp.dot(shard_rows, w_mlp_in, preferred_element_type=jnp.float32), approximate=True
    ).astype(jnp.bfloat16)
    joined = jnp.concatenate([qkv_part, mlp_part], axis=1)
    qkv_cols = joined[:, :qkv_width]
    mlp_act = joined[:, qkv_width:]
    ys, xs = lax.axis_size("y"), lax.axis_size("x")
    by_token = lax.all_to_all(qkv_cols, ("y", "x", "zh"), split_axis=0, concat_axis=1, tiled=True)
    by_token = by_token.reshape(block_rows, ys, xs, 2, -1).swapaxes(2, 3).reshape(block_rows, -1)
    group = ("zl", "zh")
    heads_in = lax.all_to_all(by_token, group, split_axis=1, concat_axis=0, tiled=True)
    query_rows = heads_in.shape[0]
    heads4 = heads_in.reshape(query_rows, local_heads, 3, head_size)
    core_at, y_at, x_at = lax.axis_index("core"), lax.axis_index("y"), lax.axis_index("x")
    digits = (lax.axis_size("zl"), 2, ys, 2, xs, block_rows)
    token_grid = jnp.arange(seq_count * tok_seq, dtype=jnp.int32).reshape(digits)

    def own_queries(grid):
        grid = lax.dynamic_index_in_dim(grid, core_at, axis=1, keepdims=False)
        grid = lax.dynamic_index_in_dim(grid, y_at, axis=1, keepdims=False)
        grid = lax.dynamic_index_in_dim(grid, x_at, axis=2, keepdims=False)
        return grid.reshape((query_rows,) + grid.shape[3:])

    query_ids = own_queries(token_grid)
    query_request = segment_of(query_ids, request_ends)
    angles = angles_of(own_queries(positions.reshape(digits + (-1,))), rope_table(head_size))
    query_rot = rotate(rms_scale(heads4[:, :, 0].astype(jnp.float32), q_gain), angles).astype(
        jnp.bfloat16
    )
    key_rot = rotate(rms_scale(heads4[:, :, 1].astype(jnp.float32), k_gain), angles).astype(
        jnp.bfloat16
    )
    value_rows = heads4[:, :, 2]
    kv_rows = jnp.concatenate([key_rot, value_rows], axis=2)
    key_order = (1, 2, 4, 0, 3, 5)
    key_ids = token_grid.transpose(key_order).reshape(-1)
    key_request = segment_of(key_ids, request_ends)
    kept = key_keep.reshape(digits).transpose(key_order).reshape(-1) == 1
    visible = (query_request[:, None] == key_request[None, :]) & (
        kept[None, :] | (query_ids[:, None] == key_ids[None, :])
    )
    first_core = core_at == 0
    head_out = []
    got = lax.all_to_all(
        jnp.broadcast_to(kv_rows[None], (ys * xs,) + kv_rows.shape), PLANE, 0, 0, tiled=True
    )
    sibling = lax.ppermute(got, "core", SWAP)
    both = jnp.stack([jnp.where(first_core, got, sibling), jnp.where(first_core, sibling, got)])
    both = both.reshape((-1,) + kv_rows.shape[1:])
    for head in range(local_heads):
        key_h = both[:, head, :head_size]
        value_h = both[:, head, head_size:]
        scores = (
            jnp.einsum("qd,kd->qk", query_rot[:, head], key_h, preferred_element_type=jnp.float32)
            * inv_root
        )
        row_high = jnp.max(jnp.where(visible, scores, -1e30), axis=1)
        weights = jnp.where(visible, jnp.exp(scores - row_high[:, None]), 0.0)
        totals = jnp.sum(weights, axis=1)
        mixed = jnp.dot(weights.astype(jnp.bfloat16), value_h, preferred_element_type=jnp.float32)
        head_out.append((mixed / totals[:, None]).astype(jnp.bfloat16))
    attended = jnp.stack(head_out, axis=1)
    attended = attended.reshape(query_rows, local_heads * head_size)
    attn_feats = lax.all_to_all(attended, group, split_axis=0, concat_axis=1, tiled=True)
    attn_feats = attn_feats.reshape(block_rows, ys, 2, xs, -1).swapaxes(2, 3).reshape(block_rows, -1)
    attn_local = lax.all_to_all(attn_feats, ("y", "x", "zh"), split_axis=1, concat_axis=0, tiled=True)
    mlp_out = jnp.dot(mlp_act, w_mlp_out, preferred_element_type=jnp.float32)
    partial = (jnp.dot(attn_local, w_attn_out, preferred_element_type=jnp.float32) + mlp_out).astype(
        jnp.bfloat16
    )
    summed = reduce_blk(partial)
    return stream + mod_gate * summed


def solution(mesh):
    zl = mesh.shape["seq"] // 2
    ys, xs = 4, mesh.shape["blk"] // 8
    fine = jax.sharding.Mesh(mesh.devices.reshape(zl, 2, ys, 2, xs), SEQ + BLK)
    in_specs = (
        P(SEQ + BLK, None),
        P(),
        P(),
        P(),
        P(),
        P(),
        P(None, BLK),
        P(None, BLK),
        P(),
        P(),
        P(BLK, None),
        P(BLK, None),
    )
    out_specs = P(SEQ + BLK, None)
    return jax.shard_map(body, mesh=fine, in_specs=in_specs, out_specs=out_specs, check_vma=False)
```
